256 devices in a mesh: zone: 8 (over x, z_lo), brick: 32 (over z_hi, y, core).
Axes of the slice: x: 4, y: 4, z: 8 (z_hi: 4, z_lo: 2; z = z_hi * 2 + z_lo), core: 2. Of those that a mesh axis runs over, the one named last changes fastest.
Arguments:
- velocity: float32 [3, 2048, 64, 256], P(None, ('zone', 'brick')), may hold values from -3 to 3
- enthalpy: float32 [2048, 64, 256], P(('zone', 'brick')), may hold values from -6 to 6
- solvent: float32 [2048, 64, 256], P(('zone', 'brick')), may hold values from 0 to 1
- pressure: float32 [2048, 64, 256], P(('zone', 'brick')), may hold values from -6 to 6
- porosity: float32 [2048, 64, 256], P(('zone', 'brick')), may hold values from 0.1 to 1
- solid_mask: int32 [2048, 64, 256], P(('zone', 'brick')), may hold values 0 or 1
- nozzle_mask: int32 [2048, 256], P(('zone', 'brick')), may hold values 0 or 1
- zone_sizes: int32 [8], replicated, may hold values from 16 to 64, as said below
- zone_setpoint: float32 [8], replicated, may hold values from 0.5 to 2
- duct_source: int32 [256], P(('zone', 'brick')), may hold values from 0 to 7
- duct_span: int32 [256, 2], P(('zone', 'brick')), may hold values from 0 to 256, as said below
Outputs:
- velocity_new: float32 [3, 2048, 64, 256], P(None, ('zone', 'brick'))
- enthalpy_new: float32 [2048, 64, 256], P(('zone', 'brick'))
- solvent_new: float32 [2048, 64, 256], P(('zone', 'brick'))
- pressure_new: float32 [2048, 64, 256], P(('zone', 'brick'))
The draws below stay inside these ranges and needn't reach their ends.
Inputs may be any that keep to these rules, and one draw needn't show every extreme that they name: `zone_sizes`: each zone's group holds a multiple of one thirty-second of all devices; the groups cover all devices, zone 0 first. duct_span[d,0] + duct_span[d,1] <= 256; duct_span[d,1] >= 64.
All inputs are finite; a program needn't handle non-finite values. No bound on the sum of `solid_mask` or of `nozzle_mask` on one device may be relied on, other than what follows from the above.
Results may differ from the reference program's by a relative error of at most 0.0003.
Values sent between devices are 32-bit elements; how exact they have to be, the bound alone decides.
No kernel may reach another device: no remote copies, remote signals or barrier semaphores. Data moves between devices by JAX's collectives and lax.ppermute only.
A program may use at most 128 MiB of HBM per device.

```python
import math
import jax
import jax.numpy as jnp
from jax import lax

CX = 8
NY = 64
NZ = 256
ITERS = 4
NZONES = 8
NX = 2048
N_ZONE = 8
N_BRICK = 32


def draw_solvent(key, part):
    base_key, level_key = jax.random.split(jax.random.fold_in(key, 5), 2)
    base = jax.random.uniform(base_key, (NX, NY, NZ), jnp.float32)
    levels = jnp.exp(jax.random.uniform(level_key, (NX // CX,), jnp.float32, -1.2, 0.0))
    level_rows = jnp.repeat(levels, CX)
    along = jnp.arange(NX, dtype=jnp.float32) / NX
    ramp = (3.0 - 2.0 * along) / 3.0
    return base * (ramp * level_rows)[:, None, None]


def draw_zone_sizes(key, part):
    unit = N_ZONE * N_BRICK // 32
    first_key, second_key, third_key = jax.random.split(jax.random.fold_in(key, 11), 3)
    pairs = jax.random.randint(first_key, (2,), 0, 4)
    single = jax.random.randint(second_key, (1,), 0, 5)
    extras = jnp.concatenate([jnp.array([0, 6], jnp.int32), pairs, 3 - pairs, single, 4 - single]).astype(jnp.int32)
    order = jax.random.permutation(third_key, 8)
    return ((2 + extras[order]) * unit).astype(jnp.int32)


def draw_duct_span(key, part):
    devices = N_ZONE * N_BRICK
    first_key, second_key, third_key = jax.random.split(jax.random.fold_in(key, 23), 3)
    widths = jax.random.randint(first_key, (devices,), NZ // 4, NZ + 1)
    chosen = jax.random.randint(second_key, (), 0, devices)
    widths = jnp.where(jnp.arange(devices) == chosen, NZ, widths).astype(jnp.int32)
    offsets = jax.random.randint(third_key, (devices,), 0, NZ - widths + 1).astype(jnp.int32)
    return jnp.stack([offsets, widths], axis=1)


def with_ends(values, stream_key, smallest, top_value):
    shape = values.shape
    spot = [jax.random.randint(jax.random.fold_in(stream_key, axis), (), 0, shape[axis]) for axis in range(len(shape))]
    values = values.at[tuple(spot)].set(smallest)
    longest = shape.index(max(shape))
    spot[longest] = (spot[longest] + 1) % shape[longest]
    return values.at[tuple(spot)].set(top_value)


def block_levels(rng, dims, cuts, low, high):
    level, own = 1.0, jax.random.fold_in(rng, 6)
    for position, shards_of in cuts:
        draws = jnp.exp(jax.random.uniform(jax.random.fold_in(own, position), (shards_of,), jnp.float32, low / len(cuts), high / len(cuts)))
        level = level * jnp.repeat(draws, dims[position] // shards_of).reshape([-1 if axis == position else 1 for axis in range(len(dims))])
    return level


def bell_draw(own_key, extent, spread, reach, cuts=(), kind=jnp.bfloat16):
    loudness = block_levels(own_key, extent, cuts, -0.22, 0.18) if cuts else 1.0
    values = jax.random.normal(own_key, extent, jnp.float32) * spread * loudness
    return jnp.minimum(jnp.maximum(values, -reach), reach).astype(kind)


def setup_inputs(seed: int = 0) -> dict:
    arg_keys = jax.random.split(jax.random.key(seed), 12)
    return {
        "velocity": bell_draw(arg_keys[0], (3, NX, NY, NZ), 0.7, 3.0, ((1, 256),), jnp.float32),
        "enthalpy": bell_draw(arg_keys[1], (NX, NY, NZ), 1.0, 6.0, ((0, 256),), jnp.float32),
        "solvent": draw_solvent(jax.random.fold_in(arg_keys[11], 71), 0),
        "pressure": bell_draw(arg_keys[3], (NX, NY, NZ), 1.0, 6.0, ((0, 256),), jnp.float32),
        "porosity": jnp.clip(jnp.exp(math.log(1.0) - 2.3025851 * jax.random.uniform(arg_keys[4], (NX, NY, NZ), jnp.float32) ** block_levels(arg_keys[4], (NX, NY, NZ), ((0, 256),), -0.2, 0.2)), 0.1, 1.0),
        "solid_mask": with_ends((jax.random.randint(arg_keys[5], (NX, NY, NZ), 0, 4) < 1).astype(jnp.int32), jax.random.fold_in(arg_keys[5], 1), 0, 1),
        "nozzle_mask": with_ends((jax.random.randint(arg_keys[6], (NX, NZ), 0, 2) < 1).astype(jnp.int32), jax.random.fold_in(arg_keys[6], 1), 0, 1),
        "zone_sizes": draw_zone_sizes(jax.random.fold_in(arg_keys[11], 71), 0),
        "zone_setpoint": jnp.clip(jax.random.uniform(arg_keys[8], (NZONES,), jnp.float32, 0.5, 2.0), 0.5, 2.0),
        "duct_source": with_ends(jax.random.randint(arg_keys[9], (N_ZONE * N_BRICK,), 0, N_ZONE), jax.random.fold_in(arg_keys[9], 1), 0, N_ZONE - 1).astype(jnp.int32),
        "duct_span": draw_duct_span(jax.random.fold_in(arg_keys[11], 71), 0),
    }


time_step = 0.2
viscosity = 0.1
diffusivity = 0.1
buoyancy = 0.5
evaporation = 0.5
latent_heat = 0.8
solvent_limit = 0.2


def shifted_down(values, axis):
    border = jnp.zeros_like(lax.slice_in_dim(values, 0, 1, axis=axis))
    inner = lax.slice_in_dim(values, 0, values.shape[axis] - 1, axis=axis)
    return jnp.concatenate([border, inner], axis=axis)


def shifted_up(values, axis):
    border = jnp.zeros_like(lax.slice_in_dim(values, 0, 1, axis=axis))
    inner = lax.slice_in_dim(values, 1, values.shape[axis], axis=axis)
    return jnp.concatenate([inner, border], axis=axis)


def momentum(vel_ext, pres_ext, heat_ext, poro_ext):
    open_here = poro_ext[1:-1]
    pressure_mid = pres_ext[1:-1]
    parts = []
    for component in range(3):
        values = vel_ext[component]
        centre = values[1:-1]
        laplacian = values[:-2] + values[2:] + shifted_down(centre, 1) + shifted_up(centre, 1)
        laplacian = laplacian + shifted_down(centre, 2) + shifted_up(centre, 2) - 6.0 * centre
        if component == 0:
            gradient = 0.5 * (pres_ext[2:] - pres_ext[:-2])
        else:
            gradient = 0.5 * (shifted_up(pressure_mid, component) - shifted_down(pressure_mid, component))
        forcing = viscosity * laplacian - gradient
        if component == 1:
            forcing = forcing + buoyancy * heat_ext[1:-1]
        parts.append(open_here * (centre + time_step * forcing))
    return jnp.stack(parts)


def divergence(star_ext):
    result = 0.5 * (star_ext[0, 2:] - star_ext[0, :-2])
    middle = star_ext[1, 1:-1]
    result = result + 0.5 * (shifted_up(middle, 1) - shifted_down(middle, 1))
    across = star_ext[2, 1:-1]
    return result + 0.5 * (shifted_up(across, 2) - shifted_down(across, 2))


def transport(scalar_ext, vel_star):
    centre = scalar_ext[1:-1]
    laplacian = scalar_ext[:-2] + scalar_ext[2:] + shifted_down(centre, 1) + shifted_up(centre, 1)
    laplacian = laplacian + shifted_down(centre, 2) + shifted_up(centre, 2) - 6.0 * centre
    advect = jnp.maximum(vel_star[0], 0.0) * (centre - scalar_ext[:-2]) + jnp.minimum(vel_star[0], 0.0) * (scalar_ext[2:] - centre)
    for component in (1, 2):
        advect = advect + jnp.maximum(vel_star[component], 0.0) * (centre - shifted_down(centre, component))
        advect = advect + jnp.minimum(vel_star[component], 0.0) * (shifted_up(centre, component) - centre)
    return centre + time_step * (diffusivity * laplacian - advect)


def sweep(pres_ext, open_ext, source):
    open_here = open_ext[1:-1]
    pressure_mid = pres_ext[1:-1]
    face_back = 0.5 * (open_here + open_ext[:-2])
    face_front = 0.5 * (open_here + open_ext[2:])
    numerator = face_back * pres_ext[:-2] + face_front * pres_ext[2:] - source
    denominator = face_back + face_front
    for component in (1, 2):
        face_low = 0.5 * (open_here + shifted_down(open_here, component))
        face_high = 0.5 * (open_here + shifted_up(open_here, component))
        numerator = numerator + face_low * shifted_down(pressure_mid, component) + face_high * shifted_up(pressure_mid, component)
        denominator = denominator + face_low + face_high
    inside = open_here > 0.0
    return jnp.where(inside, numerator / jnp.where(inside, denominator, 1.0), 0.0)


def widen(values, axis):
    widths = [(0, 0)] * values.ndim
    widths[axis] = (1, 1)
    return jnp.pad(values, widths)


def reference(velocity, enthalpy, solvent, pressure, porosity, solid_mask, nozzle_mask, zone_sizes, zone_setpoint, duct_source, duct_span):
    vel_star = momentum(widen(velocity, 1), widen(pressure, 0), widen(enthalpy, 0), widen(porosity, 0))
    source = divergence(widen(vel_star, 1)) / time_step
    heat_new = transport(widen(enthalpy, 0), vel_star)
    solv_new = transport(widen(solvent, 0), vel_star)
    drying = time_step * evaporation * solid_mask.astype(jnp.float32) * solvent
    heat_new = heat_new - latent_heat * drying
    solv_new = solv_new - drying
    devices = N_ZONE * N_BRICK
    starts = jnp.cumsum(zone_sizes) - zone_sizes
    device_ids = jnp.arange(devices, dtype=jnp.int32)
    zone_of = jnp.sum((device_ids[:, None] >= starts[None, :]).astype(jnp.int32), axis=1) - 1
    choose = (zone_of[:, None] == jnp.arange(NZONES, dtype=jnp.int32)[None, :]).astype(jnp.float32)
    top_heat = enthalpy[:, NY - 1, :].reshape(devices, CX, NZ)
    top_solv = solvent[:, NY - 1, :].reshape(devices, CX, NZ)
    device_sums = jnp.sum(top_solv.reshape(devices, CX * NZ), axis=1)
    totals = jnp.sum(choose * device_sums[:, None], axis=0)
    counts = zone_sizes.astype(jnp.float32) * (CX * NZ)
    means = totals / counts
    fresh_all = means / (means + solvent_limit)
    fresh = jnp.sum(choose * fresh_all[None, :], axis=1)[:, None, None]
    target = jnp.sum(choose * zone_setpoint[None, :], axis=1)[:, None, None]
    sources = (duct_source * N_BRICK + device_ids % N_BRICK).astype(jnp.int32)
    duct_heat = jnp.take(top_heat, sources, axis=0)
    duct_solv = jnp.take(top_solv, sources, axis=0)
    supply_heat = ((1.0 - fresh) * duct_heat + fresh * target).reshape(NX, NZ)
    supply_solv = ((1.0 - fresh) * duct_solv).reshape(NX, NZ)
    column = jnp.arange(NZ, dtype=jnp.int32)[None, :]
    inside_box = (column >= duct_span[:, 0:1]) & (column < duct_span[:, 0:1] + duct_span[:, 1:2])
    jets = ((nozzle_mask.reshape(devices, CX, NZ) > 0) & inside_box[:, None, :]).reshape(NX, NZ)
    heat_layer = jnp.where(jets, supply_heat, heat_new[:, 0, :])
    solv_layer = jnp.where(jets, supply_solv, solv_new[:, 0, :])
    enthalpy_new = jnp.concatenate([heat_layer[:, None, :], heat_new[:, 1:, :]], axis=1)
    solvent_new = jnp.concatenate([solv_layer[:, None, :], solv_new[:, 1:, :]], axis=1)
    open_ext = widen(porosity, 0)
    iterate = pressure
    for iteration in range(ITERS):
        iterate = sweep(widen(iterate, 0), open_ext, source)
    pres_ext = widen(iterate, 0)
    gradients = jnp.stack([0.5 * (pres_ext[2:] - pres_ext[:-2]), 0.5 * (shifted_up(iterate, 1) - shifted_down(iterate, 1)), 0.5 * (shifted_up(iterate, 2) - shifted_down(iterate, 2))])
    velocity_new = vel_star - time_step * porosity[None] * gradients
    return velocity_new, enthalpy_new, solvent_new, iterate
```

```python
import jax
import jax.numpy as jnp
from jax import lax
from jax.sharding import PartitionSpec as P

ITERS = 4
ALL = ("zone", "brick")
REDUCE_SLOTS = 16384


time_step = 0.2
viscosity = 0.1
diffusivity = 0.1
buoyancy = 0.5
evaporation = 0.5
latent_heat = 0.8
solvent_limit = 0.2


def neighbours(head, tail):
    count = lax.axis_size(ALL)
    from_left = lax.ppermute(tail, ALL, [(i, i + 1) for i in range(count - 1)])
    from_right = lax.ppermute(head, ALL, [(i + 1, i) for i in range(count - 1)])
    return from_left, from_right


def shifted_down(values, axis):
    border = jnp.zeros_like(lax.slice_in_dim(values, 0, 1, axis=axis))
    inner = lax.slice_in_dim(values, 0, values.shape[axis] - 1, axis=axis)
    return jnp.concatenate([border, inner], axis=axis)


def shifted_up(values, axis):
    border = jnp.zeros_like(lax.slice_in_dim(values, 0, 1, axis=axis))
    inner = lax.slice_in_dim(values, 1, values.shape[axis], axis=axis)
    return jnp.concatenate([inner, border], axis=axis)


def momentum(vel2, pres5, heat1, poro5):
    open_here = poro5[4:14]
    pressure_mid = pres5[4:14]
    parts = []
    for component in range(3):
        values = vel2[component]
        centre = values[1:-1]
        laplacian = values[:-2] + values[2:] + shifted_down(centre, 1) + shifted_up(centre, 1)
        laplacian = laplacian + shifted_down(centre, 2) + shifted_up(centre, 2) - 6.0 * centre
        if component == 0:
            gradient = 0.5 * (pres5[5:15] - pres5[3:13])
        else:
            gradient = 0.5 * (
                shifted_up(pressure_mid, component) - shifted_down(pressure_mid, component)
            )
        forcing = viscosity * laplacian - gradient
        if component == 1:
            forcing = forcing + buoyancy * heat1
        parts.append(open_here * (centre + time_step * forcing))
    return parts


def divergence(star):
    result = 0.5 * (star[0][2:] - star[0][:-2])
    middle = star[1][1:-1]
    result = result + 0.5 * (shifted_up(middle, 1) - shifted_down(middle, 1))
    across = star[2][1:-1]
    return result + 0.5 * (shifted_up(across, 2) - shifted_down(across, 2))


def transport(scalar_ext, vel_star):
    centre = scalar_ext[1:-1]
    laplacian = scalar_ext[:-2] + scalar_ext[2:] + shifted_down(centre, 1) + shifted_up(centre, 1)
    laplacian = laplacian + shifted_down(centre, 2) + shifted_up(centre, 2) - 6.0 * centre
    advect = jnp.maximum(vel_star[0], 0.0) * (centre - scalar_ext[:-2]) + jnp.minimum(
        vel_star[0], 0.0
    ) * (scalar_ext[2:] - centre)
    for component in (1, 2):
        advect = advect + jnp.maximum(vel_star[component], 0.0) * (
            centre - shifted_down(centre, component)
        )
        advect = advect + jnp.minimum(vel_star[component], 0.0) * (
            shifted_up(centre, component) - centre
        )
    return centre + time_step * (diffusivity * laplacian - advect)


def sweep(pres_ext, open_ext, source):
    open_here = open_ext[1:-1]
    pressure_mid = pres_ext[1:-1]
    face_back = 0.5 * (open_here + open_ext[:-2])
    face_front = 0.5 * (open_here + open_ext[2:])
    numerator = face_back * pres_ext[:-2] + face_front * pres_ext[2:] - source
    denominator = face_back + face_front
    for component in (1, 2):
        face_low = 0.5 * (open_here + shifted_down(open_here, component))
        face_high = 0.5 * (open_here + shifted_up(open_here, component))
        numerator = (
            numerator
            + face_low * shifted_down(pressure_mid, component)
            + face_high * shifted_up(pressure_mid, component)
        )
        denominator = denominator + face_low + face_high
    inside = open_here > 0.0
    return jnp.where(inside, numerator / jnp.where(inside, denominator, 1.0), 0.0)


def on_device_body(
    velocity,
    enthalpy,
    solvent,
    pressure,
    porosity,
    solid_mask,
    nozzle_mask,
    zone_sizes,
    zone_setpoint,
    duct_source,
    duct_span,
):
    cx = enthalpy.shape[0]
    device = lax.axis_index(ALL)

    starts = jnp.cumsum(zone_sizes) - zone_sizes
    zone_here = jnp.sum((device >= starts).astype(jnp.int32)) - 1
    nzones = zone_sizes.shape[0]
    choose = (jnp.arange(nzones, dtype=jnp.int32) == zone_here).astype(jnp.float32)
    mine = choose * jnp.sum(solvent[:, -1, :])
    slots = jnp.zeros((REDUCE_SLOTS,), jnp.float32).at[:nzones].set(mine)
    totals = lax.psum(slots, ALL)[:nzones]

    planes = jnp.stack([enthalpy[:, -1, :], solvent[:, -1, :]])
    rows = lax.axis_size("zone")
    buffer = jnp.zeros((rows,) + planes.shape, jnp.float32)
    buffer = lax.dynamic_update_slice(
        buffer, planes[None], (lax.axis_index("zone"), 0, 0, 0)
    )
    gathered = lax.psum(buffer, "zone")

    narrow_head = jnp.concatenate(
        [velocity[:, 0:2].reshape((6,) + enthalpy.shape[1:]), pressure[0:2],
         enthalpy[0:1], solvent[0:1]], axis=0)
    narrow_tail = jnp.concatenate(
        [velocity[:, cx - 2:].reshape((6,) + enthalpy.shape[1:]), pressure[cx - 2:],
         enthalpy[cx - 1:], solvent[cx - 1:]], axis=0)
    wide_head = jnp.concatenate([pressure[0:5], porosity[0:5]], axis=0)
    wide_tail = jnp.concatenate([pressure[cx - 5:], porosity[cx - 5:]], axis=0)
    n_left, n_right = neighbours(narrow_head, narrow_tail)
    w_left, w_right = neighbours(wide_head, wide_tail)

    vel2 = jnp.concatenate(
        [n_left[0:6].reshape((3, 2) + enthalpy.shape[1:]), velocity,
         n_right[0:6].reshape((3, 2) + enthalpy.shape[1:])], axis=1)
    pres5 = jnp.concatenate([w_left[0:5], pressure, w_right[0:5]], axis=0)
    poro5 = jnp.concatenate([w_left[5:10], porosity, w_right[5:10]], axis=0)
    heat1 = jnp.concatenate([n_left[8:9], enthalpy, n_right[8:9]], axis=0)
    solv1 = jnp.concatenate([n_left[9:10], solvent, n_right[9:10]], axis=0)

    star = momentum(vel2, pres5, heat1, poro5)
    source = divergence(star) / time_step
    vel_star = jnp.stack([part[1:-1] for part in star])

    s_left, s_right = neighbours(source[0:4], source[cx - 4:])
    source4 = jnp.concatenate([s_left, source, s_right], axis=0)

    heat_new = transport(heat1, vel_star)
    solv_new = transport(solv1, vel_star)
    drying = time_step * evaporation * solid_mask.astype(jnp.float32) * solvent
    heat_new = heat_new - latent_heat * drying
    solv_new = solv_new - drying

    iterate = pres5
    for iteration in range(ITERS):
        lo = iteration
        hi = poro5.shape[0] - iteration
        iterate = sweep(iterate, poro5[lo:hi], source4[lo:hi - 2])
    iterate, heat_new, solv_new, totals, gathered = lax.optimization_barrier(
        (iterate, heat_new, solv_new, totals, gathered))

    counts = zone_sizes.astype(jnp.float32) * (cx * enthalpy.shape[2])
    means = totals / counts
    fresh_all = means / (means + solvent_limit)
    fresh = jnp.sum(choose * fresh_all)
    target = jnp.sum(choose * zone_setpoint)
    arrived = lax.dynamic_index_in_dim(gathered, duct_source[0], axis=0, keepdims=False)
    supply_heat = (1.0 - fresh) * arrived[0] + fresh * target
    supply_solv = (1.0 - fresh) * arrived[1]
    column = jnp.arange(enthalpy.shape[2], dtype=jnp.int32)
    inside_box = (column >= duct_span[0, 0]) & (column < duct_span[0, 0] + duct_span[0, 1])
    jets = (nozzle_mask > 0) & inside_box[None, :]
    heat_layer = jnp.where(jets, supply_heat, heat_new[:, 0, :])
    solv_layer = jnp.where(jets, supply_solv, solv_new[:, 0, :])
    enthalpy_new = jnp.concatenate([heat_layer[:, None, :], heat_new[:, 1:, :]], axis=1)
    solvent_new = jnp.concatenate([solv_layer[:, None, :], solv_new[:, 1:, :]], axis=1)

    final = iterate[1:-1]
    gradients = jnp.stack(
        [
            0.5 * (iterate[2:] - iterate[:-2]),
            0.5 * (shifted_up(final, 1) - shifted_down(final, 1)),
            0.5 * (shifted_up(final, 2) - shifted_down(final, 2)),
        ]
    )
    velocity_new = vel_star - time_step * porosity[None] * gradients
    return (velocity_new, enthalpy_new, solvent_new, final)


def solution(mesh):
    placed = (
        P(None, ALL, None, None),
        P(ALL, None, None),
        P(ALL, None, None),
        P(ALL, None, None),
        P(ALL, None, None),
        P(ALL, None, None),
        P(ALL, None),
        P(),
        P(),
        P(ALL),
        P(ALL, None),
    )
    return jax.shard_map(
        on_device_body,
        mesh=mesh,
        in_specs=placed,
        out_specs=(
            P(None, ALL, None, None),
            P(ALL, None, None),
            P(ALL, None, None),
            P(ALL, None, None),
        ),
        check_vma=False,
    )
```

```python
import jax
import jax.numpy as jnp
from jax import lax
from jax.sharding import PartitionSpec as P

ITERS = 4
ALL = ("zone", "brick")


time_step = 0.2
viscosity = 0.1
diffusivity = 0.1
buoyancy = 0.5
evaporation = 0.5
latent_heat = 0.8
solvent_limit = 0.2


def neighbours(head, tail):
    count = lax.axis_size(ALL)
    from_left = lax.ppermute(tail, ALL, [(i, i + 1) for i in range(count - 1)])
    from_right = lax.ppermute(head, ALL, [(i + 1, i) for i in range(count - 1)])
    return from_left, from_right


def shifted_down(values, axis):
    border = jnp.zeros_like(lax.slice_in_dim(values, 0, 1, axis=axis))
    inner = lax.slice_in_dim(values, 0, values.shape[axis] - 1, axis=axis)
    return jnp.concatenate([border, inner], axis=axis)


def shifted_up(values, axis):
    border = jnp.zeros_like(lax.slice_in_dim(values, 0, 1, axis=axis))
    inner = lax.slice_in_dim(values, 1, values.shape[axis], axis=axis)
    return jnp.concatenate([inner, border], axis=axis)


def momentum(vel2, pres5, heat1, poro5):
    open_here = poro5[4:14]
    pressure_mid = pres5[4:14]
    parts = []
    for component in range(3):
        values = vel2[component]
        centre = values[1:-1]
        laplacian = values[:-2] + values[2:] + shifted_down(centre, 1) + shifted_up(centre, 1)
        laplacian = laplacian + shifted_down(centre, 2) + shifted_up(centre, 2) - 6.0 * centre
        if component == 0:
            gradient = 0.5 * (pres5[5:15] - pres5[3:13])
        else:
            gradient = 0.5 * (
                shifted_up(pressure_mid, component) - shifted_down(pressure_mid, component)
            )
        forcing = viscosity * laplacian - gradient
        if component == 1:
            forcing = forcing + buoyancy * heat1
        parts.append(open_here * (centre + time_step * forcing))
    return parts


def divergence(star):
    result = 0.5 * (star[0][2:] - star[0][:-2])
    middle = star[1][1:-1]
    result = result + 0.5 * (shifted_up(middle, 1) - shifted_down(middle, 1))
    across = star[2][1:-1]
    return result + 0.5 * (shifted_up(across, 2) - shifted_down(across, 2))


def transport(scalar_ext, vel_star):
    centre = scalar_ext[1:-1]
    laplacian = scalar_ext[:-2] + scalar_ext[2:] + shifted_down(centre, 1) + shifted_up(centre, 1)
    laplacian = laplacian + shifted_down(centre, 2) + shifted_up(centre, 2) - 6.0 * centre
    advect = jnp.maximum(vel_star[0], 0.0) * (centre - scalar_ext[:-2]) + jnp.minimum(
        vel_star[0], 0.0
    ) * (scalar_ext[2:] - centre)
    for component in (1, 2):
        advect = advect + jnp.maximum(vel_star[component], 0.0) * (
            centre - shifted_down(centre, component)
        )
        advect = advect + jnp.minimum(vel_star[component], 0.0) * (
            shifted_up(centre, component) - centre
        )
    return centre + time_step * (diffusivity * laplacian - advect)


def sweep(pres_ext, open_ext, source):
    open_here = open_ext[1:-1]
    pressure_mid = pres_ext[1:-1]
    face_back = 0.5 * (open_here + open_ext[:-2])
    face_front = 0.5 * (open_here + open_ext[2:])
    numerator = face_back * pres_ext[:-2] + face_front * pres_ext[2:] - source
    denominator = face_back + face_front
    for component in (1, 2):
        face_low = 0.5 * (open_here + shifted_down(open_here, component))
        face_high = 0.5 * (open_here + shifted_up(open_here, component))
        numerator = (
            numerator
            + face_low * shifted_down(pressure_mid, component)
            + face_high * shifted_up(pressure_mid, component)
        )
        denominator = denominator + face_low + face_high
    inside = open_here > 0.0
    return jnp.where(inside, numerator / jnp.where(inside, denominator, 1.0), 0.0)


def on_device_body(
    velocity,
    enthalpy,
    solvent,
    pressure,
    porosity,
    solid_mask,
    nozzle_mask,
    zone_sizes,
    zone_setpoint,
    duct_source,
    duct_span,
):
    cx = enthalpy.shape[0]
    device = lax.axis_index(ALL)

    starts = jnp.cumsum(zone_sizes) - zone_sizes
    zone_here = jnp.sum((device >= starts).astype(jnp.int32)) - 1
    nzones = zone_sizes.shape[0]
    choose = (jnp.arange(nzones, dtype=jnp.int32) == zone_here).astype(jnp.float32)
    totals = choose * jnp.sum(solvent[:, -1, :])
    count = lax.axis_size(ALL)
    bit = 1
    while bit < count:
        totals = totals + lax.ppermute(totals, ALL, [(i, i ^ bit) for i in range(count)])
        bit *= 2

    planes = jnp.stack([enthalpy[:, -1, :], solvent[:, -1, :]])
    rows = lax.axis_size("zone")
    buffer = jnp.zeros((rows,) + planes.shape, jnp.float32)
    buffer = lax.dynamic_update_slice(
        buffer, planes[None], (lax.axis_index("zone"), 0, 0, 0)
    )
    bit = 1
    while bit < rows:
        buffer = buffer + lax.ppermute(buffer, "zone", [(i, i ^ bit) for i in range(rows)])
        bit *= 2
    gathered = buffer

    narrow_head = jnp.concatenate(
        [velocity[:, 0:2].reshape((6,) + enthalpy.shape[1:]), pressure[0:2],
         enthalpy[0:1], solvent[0:1]], axis=0)
    narrow_tail = jnp.concatenate(
        [velocity[:, cx - 2:].reshape((6,) + enthalpy.shape[1:]), pressure[cx - 2:],
         enthalpy[cx - 1:], solvent[cx - 1:]], axis=0)
    wide_head = jnp.concatenate([pressure[0:5], porosity[0:5]], axis=0)
    wide_tail = jnp.concatenate([pressure[cx - 5:], porosity[cx - 5:]], axis=0)
    n_left, n_right = neighbours(narrow_head, narrow_tail)
    w_left, w_right = neighbours(wide_head, wide_tail)

    vel2 = jnp.concatenate(
        [n_left[0:6].reshape((3, 2) + enthalpy.shape[1:]), velocity,
         n_right[0:6].reshape((3, 2) + enthalpy.shape[1:])], axis=1)
    pres5 = jnp.concatenate([w_left[0:5], pressure, w_right[0:5]], axis=0)
    poro5 = jnp.concatenate([w_left[5:10], porosity, w_right[5:10]], axis=0)
    heat1 = jnp.concatenate([n_left[8:9], enthalpy, n_right[8:9]], axis=0)
    solv1 = jnp.concatenate([n_left[9:10], solvent, n_right[9:10]], axis=0)

    star = momentum(vel2, pres5, heat1, poro5)
    source = divergence(star) / time_step
    vel_star = jnp.stack([part[1:-1] for part in star])

    s_left, s_right = neighbours(source[0:4], source[cx - 4:])
    source4 = jnp.concatenate([s_left, source, s_right], axis=0)

    heat_new = transport(heat1, vel_star)
    solv_new = transport(solv1, vel_star)
    drying = time_step * evaporation * solid_mask.astype(jnp.float32) * solvent
    heat_new = heat_new - latent_heat * drying
    solv_new = solv_new - drying

    iterate = pres5
    for iteration in range(ITERS):
        lo = iteration
        hi = poro5.shape[0] - iteration
        iterate = sweep(iterate, poro5[lo:hi], source4[lo:hi - 2])
    iterate, heat_new, solv_new, totals, gathered = lax.optimization_barrier(
        (iterate, heat_new, solv_new, totals, gathered))

    counts = zone_sizes.astype(jnp.float32) * (cx * enthalpy.shape[2])
    means = totals / counts
    fresh_all = means / (means + solvent_limit)
    fresh = jnp.sum(choose * fresh_all)
    target = jnp.sum(choose * zone_setpoint)
    arrived = lax.dynamic_index_in_dim(gathered, duct_source[0], axis=0, keepdims=False)
    supply_heat = (1.0 - fresh) * arrived[0] + fresh * target
    supply_solv = (1.0 - fresh) * arrived[1]
    column = jnp.arange(enthalpy.shape[2], dtype=jnp.int32)
    inside_box = (column >= duct_span[0, 0]) & (column < duct_span[0, 0] + duct_span[0, 1])
    jets = (nozzle_mask > 0) & inside_box[None, :]
    heat_layer = jnp.where(jets, supply_heat, heat_new[:, 0, :])
    solv_layer = jnp.where(jets, supply_solv, solv_new[:, 0, :])
    enthalpy_new = jnp.concatenate([heat_layer[:, None, :], heat_new[:, 1:, :]], axis=1)
    solvent_new = jnp.concatenate([solv_layer[:, None, :], solv_new[:, 1:, :]], axis=1)

    final = iterate[1:-1]
    gradients = jnp.stack(
        [
            0.5 * (iterate[2:] - iterate[:-2]),
            0.5 * (shifted_up(final, 1) - shifted_down(final, 1)),
            0.5 * (shifted_up(final, 2) - shifted_down(final, 2)),
        ]
    )
    velocity_new = vel_star - time_step * porosity[None] * gradients
    return (velocity_new, enthalpy_new, solvent_new, final)


def solution(mesh):
    placed = (
        P(None, ALL, None, None),
        P(ALL, None, None),
        P(ALL, None, None),
        P(ALL, None, None),
        P(ALL, None, None),
        P(ALL, None, None),
        P(ALL, None),
        P(),
        P(),
        P(ALL),
        P(ALL, None),
    )
    return jax.shard_map(
        on_device_body,
        mesh=mesh,
        in_specs=placed,
        out_specs=(
            P(None, ALL, None, None),
            P(ALL, None, None),
            P(ALL, None, None),
            P(ALL, None, None),
        ),
        check_vma=False,
    )
```

```python
import jax
import jax.numpy as jnp
from jax import lax
from jax.sharding import PartitionSpec as P

ITERS = 4
ALL = ("zone", "brick")


time_step = 0.2
viscosity = 0.1
diffusivity = 0.1
buoyancy = 0.5
evaporation = 0.5
latent_heat = 0.8
solvent_limit = 0.2


def neighbours(head, tail):
    count = lax.axis_size(ALL)
    from_left = lax.ppermute(tail, ALL, [(i, i + 1) for i in range(count - 1)])
    from_right = lax.ppermute(head, ALL, [(i + 1, i) for i in range(count - 1)])
    return from_left, from_right


def shifted_down(values, axis):
    border = jnp.zeros_like(lax.slice_in_dim(values, 0, 1, axis=axis))
    inner = lax.slice_in_dim(values, 0, values.shape[axis] - 1, axis=axis)
    return jnp.concatenate([border, inner], axis=axis)


def shifted_up(values, axis):
    border = jnp.zeros_like(lax.slice_in_dim(values, 0, 1, axis=axis))
    inner = lax.slice_in_dim(values, 1, values.shape[axis], axis=axis)
    return jnp.concatenate([inner, border], axis=axis)


def momentum(vel2, pres5, heat1, poro5):
    open_here = poro5[4:14]
    pressure_mid = pres5[4:14]
    parts = []
    for component in range(3):
        values = vel2[component]
        centre = values[1:-1]
        laplacian = values[:-2] + values[2:] + shifted_down(centre, 1) + shifted_up(centre, 1)
        laplacian = laplacian + shifted_down(centre, 2) + shifted_up(centre, 2) - 6.0 * centre
        if component == 0:
            gradient = 0.5 * (pres5[5:15] - pres5[3:13])
        else:
            gradient = 0.5 * (
                shifted_up(pressure_mid, component) - shifted_down(pressure_mid, component)
            )
        forcing = viscosity * laplacian - gradient
        if component == 1:
            forcing = forcing + buoyancy * heat1
        parts.append(open_here * (centre + time_step * forcing))
    return parts


def divergence(star):
    result = 0.5 * (star[0][2:] - star[0][:-2])
    middle = star[1][1:-1]
    result = result + 0.5 * (shifted_up(middle, 1) - shifted_down(middle, 1))
    across = star[2][1:-1]
    return result + 0.5 * (shifted_up(across, 2) - shifted_down(across, 2))


def transport(scalar_ext, vel_star):
    centre = scalar_ext[1:-1]
    laplacian = scalar_ext[:-2] + scalar_ext[2:] + shifted_down(centre, 1) + shifted_up(centre, 1)
    laplacian = laplacian + shifted_down(centre, 2) + shifted_up(centre, 2) - 6.0 * centre
    advect = jnp.maximum(vel_star[0], 0.0) * (centre - scalar_ext[:-2]) + jnp.minimum(
        vel_star[0], 0.0
    ) * (scalar_ext[2:] - centre)
    for component in (1, 2):
        advect = advect + jnp.maximum(vel_star[component], 0.0) * (
            centre - shifted_down(centre, component)
        )
        advect = advect + jnp.minimum(vel_star[component], 0.0) * (
            shifted_up(centre, component) - centre
        )
    return centre + time_step * (diffusivity * laplacian - advect)


def sweep(pres_ext, open_ext, source):
    open_here = open_ext[1:-1]
    pressure_mid = pres_ext[1:-1]
    face_back = 0.5 * (open_here + open_ext[:-2])
    face_front = 0.5 * (open_here + open_ext[2:])
    numerator = face_back * pres_ext[:-2] + face_front * pres_ext[2:] - source
    denominator = face_back + face_front
    for component in (1, 2):
        face_low = 0.5 * (open_here + shifted_down(open_here, component))
        face_high = 0.5 * (open_here + shifted_up(open_here, component))
        numerator = (
            numerator
            + face_low * shifted_down(pressure_mid, component)
            + face_high * shifted_up(pressure_mid, component)
        )
        denominator = denominator + face_low + face_high
    inside = open_here > 0.0
    return jnp.where(inside, numerator / jnp.where(inside, denominator, 1.0), 0.0)


def on_device_body(
    velocity,
    enthalpy,
    solvent,
    pressure,
    porosity,
    solid_mask,
    nozzle_mask,
    zone_sizes,
    zone_setpoint,
    duct_source,
    duct_span,
):
    cx = enthalpy.shape[0]
    device = lax.axis_index(ALL)

    starts = jnp.cumsum(zone_sizes) - zone_sizes
    zone_here = jnp.sum((device >= starts).astype(jnp.int32)) - 1
    nzones = zone_sizes.shape[0]
    choose = (jnp.arange(nzones, dtype=jnp.int32) == zone_here).astype(jnp.float32)
    totals = choose * jnp.sum(solvent[:, -1, :])
    count = lax.axis_size(ALL)
    zone_bits = []
    bit = 1
    while bit < count:
        zone_bits.append(bit)
        bit *= 2

    planes = jnp.stack([enthalpy[:, -1, :], solvent[:, -1, :]])
    rows = lax.axis_size("zone")
    buffer = jnp.zeros((rows,) + planes.shape, jnp.float32)
    buffer = lax.dynamic_update_slice(
        buffer, planes[None], (lax.axis_index("zone"), 0, 0, 0)
    )
    duct_bits = []
    bit = 1
    while bit < rows:
        duct_bits.append(bit)
        bit *= 2
    state = {"totals": totals, "buffer": buffer}

    def advance(anchor):
        sent = {}
        if zone_bits:
            b = zone_bits.pop(0)
            sent["totals"] = lax.ppermute(
                state["totals"], ALL, [(i, i ^ b) for i in range(count)])
        if duct_bits:
            b = duct_bits.pop(0)
            sent["buffer"] = lax.ppermute(
                state["buffer"], "zone", [(i, i ^ b) for i in range(rows)])
        if sent and anchor is not None:
            sent, _ = lax.optimization_barrier((sent, anchor))
        if sent:
            for key, value in sent.items():
                state[key] = state[key] + value

    narrow_head = jnp.concatenate(
        [velocity[:, 0:2].reshape((6,) + enthalpy.shape[1:]), pressure[0:2],
         enthalpy[0:1], solvent[0:1]], axis=0)
    narrow_tail = jnp.concatenate(
        [velocity[:, cx - 2:].reshape((6,) + enthalpy.shape[1:]), pressure[cx - 2:],
         enthalpy[cx - 1:], solvent[cx - 1:]], axis=0)
    wide_head = jnp.concatenate([pressure[0:5], porosity[0:5]], axis=0)
    wide_tail = jnp.concatenate([pressure[cx - 5:], porosity[cx - 5:]], axis=0)
    n_left, n_right = neighbours(narrow_head, narrow_tail)
    w_left, w_right = neighbours(wide_head, wide_tail)

    vel2 = jnp.concatenate(
        [n_left[0:6].reshape((3, 2) + enthalpy.shape[1:]), velocity,
         n_right[0:6].reshape((3, 2) + enthalpy.shape[1:])], axis=1)
    pres5 = jnp.concatenate([w_left[0:5], pressure, w_right[0:5]], axis=0)
    poro5 = jnp.concatenate([w_left[5:10], porosity, w_right[5:10]], axis=0)
    heat1 = jnp.concatenate([n_left[8:9], enthalpy, n_right[8:9]], axis=0)
    solv1 = jnp.concatenate([n_left[9:10], solvent, n_right[9:10]], axis=0)

    advance(None)
    advance(None)
    advance(None)
    advance(None)
    star = momentum(vel2, pres5, heat1, poro5)
    advance(star[1])
    source = divergence(star) / time_step
    vel_star = jnp.stack([part[1:-1] for part in star])

    s_left, s_right = neighbours(source[0:4], source[cx - 4:])
    source4 = jnp.concatenate([s_left, source, s_right], axis=0)
    advance(source4)

    heat_new = transport(heat1, vel_star)
    solv_new = transport(solv1, vel_star)
    drying = time_step * evaporation * solid_mask.astype(jnp.float32) * solvent
    heat_new = heat_new - latent_heat * drying
    solv_new = solv_new - drying

    iterate = pres5
    for iteration in range(ITERS):
        lo = iteration
        hi = poro5.shape[0] - iteration
        iterate = sweep(iterate, poro5[lo:hi], source4[lo:hi - 2])
        if iteration in (1, 2):
            advance(iterate)
    while zone_bits or duct_bits:
        advance(iterate)
    totals = state["totals"]
    gathered = state["buffer"]
    iterate, heat_new, solv_new, totals, gathered = lax.optimization_barrier(
        (iterate, heat_new, solv_new, totals, gathered))

    counts = zone_sizes.astype(jnp.float32) * (cx * enthalpy.shape[2])
    means = totals / counts
    fresh_all = means / (means + solvent_limit)
    fresh = jnp.sum(choose * fresh_all)
    target = jnp.sum(choose * zone_setpoint)
    arrived = lax.dynamic_index_in_dim(gathered, duct_source[0], axis=0, keepdims=False)
    supply_heat = (1.0 - fresh) * arrived[0] + fresh * target
    supply_solv = (1.0 - fresh) * arrived[1]
    column = jnp.arange(enthalpy.shape[2], dtype=jnp.int32)
    inside_box = (column >= duct_span[0, 0]) & (column < duct_span[0, 0] + duct_span[0, 1])
    jets = (nozzle_mask > 0) & inside_box[None, :]
    heat_layer = jnp.where(jets, supply_heat, heat_new[:, 0, :])
    solv_layer = jnp.where(jets, supply_solv, solv_new[:, 0, :])
    enthalpy_new = jnp.concatenate([heat_layer[:, None, :], heat_new[:, 1:, :]], axis=1)
    solvent_new = jnp.concatenate([solv_layer[:, None, :], solv_new[:, 1:, :]], axis=1)

    final = iterate[1:-1]
    gradients = jnp.stack(
        [
            0.5 * (iterate[2:] - iterate[:-2]),
            0.5 * (shifted_up(final, 1) - shifted_down(final, 1)),
            0.5 * (shifted_up(final, 2) - shifted_down(final, 2)),
        ]
    )
    velocity_new = vel_star - time_step * porosity[None] * gradients
    return (velocity_new, enthalpy_new, solvent_new, final)


def solution(mesh):
    placed = (
        P(None, ALL, None, None),
        P(ALL, None, None),
        P(ALL, None, None),
        P(ALL, None, None),
        P(ALL, None, None),
        P(ALL, None, None),
        P(ALL, None),
        P(),
        P(),
        P(ALL),
        P(ALL, None),
    )
    return jax.shard_map(
        on_device_body,
        mesh=mesh,
        in_specs=placed,
        out_specs=(
            P(None, ALL, None, None),
            P(ALL, None, None),
            P(ALL, None, None),
            P(ALL, None, None),
        ),
        check_vma=False,
    )
```

```python
import jax
import jax.numpy as jnp
from jax import lax
from jax.sharding import PartitionSpec as P

ITERS = 4
ALL = ("zone", "brick")


time_step = 0.2
viscosity = 0.1
diffusivity = 0.1
buoyancy = 0.5
evaporation = 0.5
latent_heat = 0.8
solvent_limit = 0.2


def neighbours(head, tail):
    count = lax.axis_size(ALL)
    from_left = lax.ppermute(tail, ALL, [(i, i + 1) for i in range(count - 1)])
    from_right = lax.ppermute(head, ALL, [(i + 1, i) for i in range(count - 1)])
    return from_left, from_right


def shifted_down(values, axis):
    border = jnp.zeros_like(lax.slice_in_dim(values, 0, 1, axis=axis))
    inner = lax.slice_in_dim(values, 0, values.shape[axis] - 1, axis=axis)
    return jnp.concatenate([border, inner], axis=axis)


def shifted_up(values, axis):
    border = jnp.zeros_like(lax.slice_in_dim(values, 0, 1, axis=axis))
    inner = lax.slice_in_dim(values, 1, values.shape[axis], axis=axis)
    return jnp.concatenate([inner, border], axis=axis)


def momentum(vel2, pres5, heat1, poro5):
    open_here = poro5[4:14]
    pressure_mid = pres5[4:14]
    parts = []
    for component in range(3):
        values = vel2[component]
        centre = values[1:-1]
        laplacian = values[:-2] + values[2:] + shifted_down(centre, 1) + shifted_up(centre, 1)
        laplacian = laplacian + shifted_down(centre, 2) + shifted_up(centre, 2) - 6.0 * centre
        if component == 0:
            gradient = 0.5 * (pres5[5:15] - pres5[3:13])
        else:
            gradient = 0.5 * (
                shifted_up(pressure_mid, component) - shifted_down(pressure_mid, component)
            )
        forcing = viscosity * laplacian - gradient
        if component == 1:
            forcing = forcing + buoyancy * heat1
        parts.append(open_here * (centre + time_step * forcing))
    return parts


def divergence(star):
    result = 0.5 * (star[0][2:] - star[0][:-2])
    middle = star[1][1:-1]
    result = result + 0.5 * (shifted_up(middle, 1) - shifted_down(middle, 1))
    across = star[2][1:-1]
    return result + 0.5 * (shifted_up(across, 2) - shifted_down(across, 2))


def transport(scalar_ext, vel_star):
    centre = scalar_ext[1:-1]
    laplacian = scalar_ext[:-2] + scalar_ext[2:] + shifted_down(centre, 1) + shifted_up(centre, 1)
    laplacian = laplacian + shifted_down(centre, 2) + shifted_up(centre, 2) - 6.0 * centre
    advect = jnp.maximum(vel_star[0], 0.0) * (centre - scalar_ext[:-2]) + jnp.minimum(
        vel_star[0], 0.0
    ) * (scalar_ext[2:] - centre)
    for component in (1, 2):
        advect = advect + jnp.maximum(vel_star[component], 0.0) * (
            centre - shifted_down(centre, component)
        )
        advect = advect + jnp.minimum(vel_star[component], 0.0) * (
            shifted_up(centre, component) - centre
        )
    return centre + time_step * (diffusivity * laplacian - advect)


def sweep(pres_ext, open_ext, source):
    open_here = open_ext[1:-1]
    pressure_mid = pres_ext[1:-1]
    face_back = 0.5 * (open_here + open_ext[:-2])
    face_front = 0.5 * (open_here + open_ext[2:])
    numerator = face_back * pres_ext[:-2] + face_front * pres_ext[2:] - source
    denominator = face_back + face_front
    for component in (1, 2):
        face_low = 0.5 * (open_here + shifted_down(open_here, component))
        face_high = 0.5 * (open_here + shifted_up(open_here, component))
        numerator = (
            numerator
            + face_low * shifted_down(pressure_mid, component)
            + face_high * shifted_up(pressure_mid, component)
        )
        denominator = denominator + face_low + face_high
    inside = open_here > 0.0
    return jnp.where(inside, numerator / jnp.where(inside, denominator, 1.0), 0.0)


def on_device_body(
    velocity,
    enthalpy,
    solvent,
    pressure,
    porosity,
    solid_mask,
    nozzle_mask,
    zone_sizes,
    zone_setpoint,
    duct_source,
    duct_span,
):
    cx = enthalpy.shape[0]
    device = lax.axis_index(ALL)

    starts = jnp.cumsum(zone_sizes) - zone_sizes
    zone_here = jnp.sum((device >= starts).astype(jnp.int32)) - 1
    nzones = zone_sizes.shape[0]
    choose = (jnp.arange(nzones, dtype=jnp.int32) == zone_here).astype(jnp.float32)
    totals = choose * jnp.sum(solvent[:, -1, :])
    count = lax.axis_size(ALL)
    rows = lax.axis_size("zone")

    planes = jnp.stack([enthalpy[:, -1, :], solvent[:, -1, :]])
    buffer = jnp.zeros((rows + 1,) + planes.shape, jnp.float32)
    buffer = lax.dynamic_update_slice(
        buffer, planes[None], (lax.axis_index("zone"), 0, 0, 0)
    )
    buffer = buffer.at[rows, 0, 0, :nzones].set(totals)
    bricks = count // rows
    duct_bits = []
    bit = 1
    while bit < rows:
        duct_bits.append(bit)
        bit *= 2
    zone_bits = []
    bit = 1
    while bit < bricks:
        zone_bits.append(bit)
        bit *= 2
    state = {"buffer": buffer, "totals": None}

    def advance(anchor):
        if duct_bits:
            b = duct_bits.pop(0)
            key = "buffer"
            sent = lax.ppermute(
                state[key], "zone", [(i, i ^ b) for i in range(rows)])
        elif zone_bits:
            b = zone_bits.pop(0)
            key = "totals"
            if state[key] is None:
                state[key] = state["buffer"][rows, 0, 0, :nzones]
            sent = lax.ppermute(
                state[key], "brick", [(i, i ^ b) for i in range(bricks)])
        else:
            return
        if anchor is not None:
            sent, _ = lax.optimization_barrier((sent, anchor))
        state[key] = state[key] + sent

    narrow_head = jnp.concatenate(
        [velocity[:, 0:2].reshape((6,) + enthalpy.shape[1:]), pressure[0:2],
         enthalpy[0:1], solvent[0:1]], axis=0)
    narrow_tail = jnp.concatenate(
        [velocity[:, cx - 2:].reshape((6,) + enthalpy.shape[1:]), pressure[cx - 2:],
         enthalpy[cx - 1:], solvent[cx - 1:]], axis=0)
    wide_head = jnp.concatenate([pressure[0:5], porosity[0:5]], axis=0)
    wide_tail = jnp.concatenate([pressure[cx - 5:], porosity[cx - 5:]], axis=0)
    n_left, n_right = neighbours(narrow_head, narrow_tail)
    w_left, w_right = neighbours(wide_head, wide_tail)

    vel2 = jnp.concatenate(
        [n_left[0:6].reshape((3, 2) + enthalpy.shape[1:]), velocity,
         n_right[0:6].reshape((3, 2) + enthalpy.shape[1:])], axis=1)
    pres5 = jnp.concatenate([w_left[0:5], pressure, w_right[0:5]], axis=0)
    poro5 = jnp.concatenate([w_left[5:10], porosity, w_right[5:10]], axis=0)
    heat1 = jnp.concatenate([n_left[8:9], enthalpy, n_right[8:9]], axis=0)
    solv1 = jnp.concatenate([n_left[9:10], solvent, n_right[9:10]], axis=0)

    advance(None)
    advance(None)
    advance(None)
    advance(None)
    star = momentum(vel2, pres5, heat1, poro5)
    advance(star[1])
    source = divergence(star) / time_step
    vel_star = jnp.stack([part[1:-1] for part in star])

    s_left, s_right = neighbours(source[0:4], source[cx - 4:])
    source4 = jnp.concatenate([s_left, source, s_right], axis=0)
    advance(source4)

    heat_new = transport(heat1, vel_star)
    solv_new = transport(solv1, vel_star)
    drying = time_step * evaporation * solid_mask.astype(jnp.float32) * solvent
    heat_new = heat_new - latent_heat * drying
    solv_new = solv_new - drying

    iterate = pres5
    for iteration in range(ITERS):
        lo = iteration
        hi = poro5.shape[0] - iteration
        iterate = sweep(iterate, poro5[lo:hi], source4[lo:hi - 2])
        if iteration in (1, 2):
            advance(iterate)
    while zone_bits or duct_bits:
        advance(iterate)
    totals = state["totals"]
    gathered = state["buffer"][:rows]
    iterate, heat_new, solv_new, totals, gathered = lax.optimization_barrier(
        (iterate, heat_new, solv_new, totals, gathered))

    counts = zone_sizes.astype(jnp.float32) * (cx * enthalpy.shape[2])
    means = totals / counts
    fresh_all = means / (means + solvent_limit)
    fresh = jnp.sum(choose * fresh_all)
    target = jnp.sum(choose * zone_setpoint)
    arrived = lax.dynamic_index_in_dim(gathered, duct_source[0], axis=0, keepdims=False)
    supply_heat = (1.0 - fresh) * arrived[0] + fresh * target
    supply_solv = (1.0 - fresh) * arrived[1]
    column = jnp.arange(enthalpy.shape[2], dtype=jnp.int32)
    inside_box = (column >= duct_span[0, 0]) & (column < duct_span[0, 0] + duct_span[0, 1])
    jets = (nozzle_mask > 0) & inside_box[None, :]
    heat_layer = jnp.where(jets, supply_heat, heat_new[:, 0, :])
    solv_layer = jnp.where(jets, supply_solv, solv_new[:, 0, :])
    enthalpy_new = jnp.concatenate([heat_layer[:, None, :], heat_new[:, 1:, :]], axis=1)
    solvent_new = jnp.concatenate([solv_layer[:, None, :], solv_new[:, 1:, :]], axis=1)

    final = iterate[1:-1]
    gradients = jnp.stack(
        [
            0.5 * (iterate[2:] - iterate[:-2]),
            0.5 * (shifted_up(final, 1) - shifted_down(final, 1)),
            0.5 * (shifted_up(final, 2) - shifted_down(final, 2)),
        ]
    )
    velocity_new = vel_star - time_step * porosity[None] * gradients
    return (velocity_new, enthalpy_new, solvent_new, final)


def solution(mesh):
    placed = (
        P(None, ALL, None, None),
        P(ALL, None, None),
        P(ALL, None, None),
        P(ALL, None, None),
        P(ALL, None, None),
        P(ALL, None, None),
        P(ALL, None),
        P(),
        P(),
        P(ALL),
        P(ALL, None),
    )
    return jax.shard_map(
        on_device_body,
        mesh=mesh,
        in_specs=placed,
        out_specs=(
            P(None, ALL, None, None),
            P(ALL, None, None),
            P(ALL, None, None),
            P(ALL, None, None),
        ),
        check_vma=False,
    )
```

```python
import jax
import jax.numpy as jnp
from jax import lax
from jax.experimental import pallas as pl
from jax.experimental.pallas import tpu as pltpu
from jax.sharding import PartitionSpec as P

ITERS = 4
ALL = ("zone", "brick")


time_step = 0.2
viscosity = 0.1
diffusivity = 0.1
buoyancy = 0.5
evaporation = 0.5
latent_heat = 0.8
solvent_limit = 0.2


def neighbours(head, tail):
    count = lax.axis_size(ALL)
    from_left = lax.ppermute(tail, ALL, [(i, i + 1) for i in range(count - 1)])
    from_right = lax.ppermute(head, ALL, [(i + 1, i) for i in range(count - 1)])
    return from_left, from_right


def _down(v, axis):
    idx = lax.broadcasted_iota(jnp.int32, v.shape, axis)
    return jnp.where(idx == 0, 0.0, pltpu.roll(v, 1, axis))


def _up(v, axis):
    n = v.shape[axis]
    idx = lax.broadcasted_iota(jnp.int32, v.shape, axis)
    return jnp.where(idx == n - 1, 0.0, pltpu.roll(v, n - 1, axis))


def _laplacian_plane(back, centre, front):
    lap = back + front + _down(centre, 0) + _up(centre, 0)
    return lap + _down(centre, 1) + _up(centre, 1) - 6.0 * centre


def stage_one_kernel(vel2, pres5, heat1, poro5, solv1, solid,
                     star_out, source_out, heat_out, solv_out, star):
    wide = star.shape[1]
    cells = source_out.shape[0]

    def momentum_plane(j, carry):
        open_here = poro5[j + 4]
        pressure_mid = pres5[j + 4]
        for component in range(3):
            centre = vel2[component, j + 1]
            laplacian = _laplacian_plane(vel2[component, j], centre, vel2[component, j + 2])
            if component == 0:
                gradient = 0.5 * (pres5[j + 5] - pres5[j + 3])
            else:
                axis = component - 1
                gradient = 0.5 * (_up(pressure_mid, axis) - _down(pressure_mid, axis))
            forcing = viscosity * laplacian - gradient
            if component == 1:
                forcing = forcing + buoyancy * heat1[j]
            star[component, j] = open_here * (centre + time_step * forcing)
        return carry

    lax.fori_loop(0, wide, momentum_plane, 0)

    def cell_plane(x, carry):
        j = x + 1
        s0 = star[0, j]
        s1 = star[1, j]
        s2 = star[2, j]
        result = 0.5 * (star[0, j + 1] - star[0, j - 1])
        result = result + 0.5 * (_up(s1, 0) - _down(s1, 0))
        result = result + 0.5 * (_up(s2, 1) - _down(s2, 1))
        source_out[x] = result / time_step
        star_out[0, x] = s0
        star_out[1, x] = s1
        star_out[2, x] = s2
        drying = time_step * evaporation * solid[x].astype(jnp.float32) * solv1[j]
        for scalar, out, latent in ((heat1, heat_out, True), (solv1, solv_out, False)):
            back = scalar[x]
            centre = scalar[j]
            front = scalar[x + 2]
            laplacian = _laplacian_plane(back, centre, front)
            advect = jnp.maximum(s0, 0.0) * (centre - back) + jnp.minimum(s0, 0.0) * (front - centre)
            advect = advect + jnp.maximum(s1, 0.0) * (centre - _down(centre, 0))
            advect = advect + jnp.minimum(s1, 0.0) * (_up(centre, 0) - centre)
            advect = advect + jnp.maximum(s2, 0.0) * (centre - _down(centre, 1))
            advect = advect + jnp.minimum(s2, 0.0) * (_up(centre, 1) - centre)
            moved = centre + time_step * (diffusivity * laplacian - advect)
            if latent:
                out[x] = moved - latent_heat * drying
            else:
                out[x] = moved - drying
        return carry

    lax.fori_loop(0, cells, cell_plane, 0)


def stage_two_kernel(pres5, poro5, source4, star_in, vel_out, pres_out, even, odd):
    cells = pres_out.shape[0]
    buffers = (even, odd)
    prev = pres5
    for k in range(ITERS):
        out = buffers[k % 2]
        count = source4.shape[0] - 2 * k

        def body(j, carry, k=k, prev=prev, out=out):
            open_here = poro5[k + j + 1]
            pressure_mid = prev[j + 1]
            face_back = 0.5 * (open_here + poro5[k + j])
            face_front = 0.5 * (open_here + poro5[k + j + 2])
            numerator = face_back * prev[j] + face_front * prev[j + 2] - source4[k + j]
            denominator = face_back + face_front
            for axis in (0, 1):
                face_low = 0.5 * (open_here + _down(open_here, axis))
                face_high = 0.5 * (open_here + _up(open_here, axis))
                numerator = (
                    numerator
                    + face_low * _down(pressure_mid, axis)
                    + face_high * _up(pressure_mid, axis)
                )
                denominator = denominator + face_low + face_high
            inside = open_here > 0.0
            out[j] = jnp.where(inside, numerator / jnp.where(inside, denominator, 1.0), 0.0)
            return carry

        lax.fori_loop(0, count, body, 0)
        prev = out
    final = prev

    def finish(x, carry):
        here = final[x + 1]
        pres_out[x] = here
        scale = time_step * poro5[x + 5]
        vel_out[0, x] = star_in[0, x] - scale * (0.5 * (final[x + 2] - final[x]))
        vel_out[1, x] = star_in[1, x] - scale * (0.5 * (_up(here, 0) - _down(here, 0)))
        vel_out[2, x] = star_in[2, x] - scale * (0.5 * (_up(here, 1) - _down(here, 1)))
        return carry

    lax.fori_loop(0, cells, finish, 0)


def _params():
    return pltpu.CompilerParams(vmem_limit_bytes=48 * 1024 * 1024)


def stage_one(vel2, pres5, heat1, poro5, solv1, solid):
    cells = solid.shape[0]
    plane = solid.shape[1:]
    f32 = jnp.float32
    outs = (
        jax.ShapeDtypeStruct((3, cells) + plane, f32),
        jax.ShapeDtypeStruct((cells,) + plane, f32),
        jax.ShapeDtypeStruct((cells,) + plane, f32),
        jax.ShapeDtypeStruct((cells,) + plane, f32),
    )
    points = cells * plane[0] * plane[1]
    return pl.pallas_call(
        stage_one_kernel,
        out_shape=outs,
        scratch_shapes=[pltpu.VMEM((3, cells + 2) + plane, f32)],
        compiler_params=_params(),
        cost_estimate=pl.CostEstimate(
            flops=260 * points, transcendentals=0, bytes_accessed=4 * points * 19),
    )(vel2, pres5, heat1, poro5, solv1, solid)


def stage_two(pres5, poro5, source4, vel_star):
    cells = vel_star.shape[1]
    plane = vel_star.shape[2:]
    f32 = jnp.float32
    outs = (
        jax.ShapeDtypeStruct((3, cells) + plane, f32),
        jax.ShapeDtypeStruct((cells,) + plane, f32),
    )
    points = cells * plane[0] * plane[1]
    return pl.pallas_call(
        stage_two_kernel,
        out_shape=outs,
        scratch_shapes=[pltpu.VMEM((source4.shape[0],) + plane, f32)] * 2,
        compiler_params=_params(),
        cost_estimate=pl.CostEstimate(
            flops=200 * points, transcendentals=0, bytes_accessed=4 * points * 12),
    )(pres5, poro5, source4, vel_star)


def on_device_body(
    velocity,
    enthalpy,
    solvent,
    pressure,
    porosity,
    solid_mask,
    nozzle_mask,
    zone_sizes,
    zone_setpoint,
    duct_source,
    duct_span,
):
    cx = enthalpy.shape[0]
    device = lax.axis_index(ALL)

    starts = jnp.cumsum(zone_sizes) - zone_sizes
    zone_here = jnp.sum((device >= starts).astype(jnp.int32)) - 1
    nzones = zone_sizes.shape[0]
    choose = (jnp.arange(nzones, dtype=jnp.int32) == zone_here).astype(jnp.float32)
    totals = choose * jnp.sum(solvent[:, -1, :])
    count = lax.axis_size(ALL)
    rows = lax.axis_size("zone")

    planes = jnp.stack([enthalpy[:, -1, :], solvent[:, -1, :]])
    buffer = jnp.zeros((rows + 1,) + planes.shape, jnp.float32)
    buffer = lax.dynamic_update_slice(
        buffer, planes[None], (lax.axis_index("zone"), 0, 0, 0)
    )
    buffer = buffer.at[rows, 0, 0, :nzones].set(totals)
    bricks = count // rows
    duct_bits = []
    bit = 1
    while bit < rows:
        duct_bits.append(bit)
        bit *= 2
    zone_bits = []
    bit = 1
    while bit < bricks:
        zone_bits.append(bit)
        bit *= 2
    state = {"buffer": buffer, "totals": None}

    def advance(anchor):
        if duct_bits:
            b = duct_bits.pop(0)
            key = "buffer"
            sent = lax.ppermute(
                state[key], "zone", [(i, i ^ b) for i in range(rows)])
        elif zone_bits:
            b = zone_bits.pop(0)
            key = "totals"
            if state[key] is None:
                state[key] = state["buffer"][rows, 0, 0, :nzones]
            sent = lax.ppermute(
                state[key], "brick", [(i, i ^ b) for i in range(bricks)])
        else:
            return
        if anchor is not None:
            sent, _ = lax.optimization_barrier((sent, anchor))
        state[key] = state[key] + sent

    narrow_head = jnp.concatenate(
        [velocity[:, 0:2].reshape((6,) + enthalpy.shape[1:]), pressure[0:2],
         enthalpy[0:1], solvent[0:1]], axis=0)
    narrow_tail = jnp.concatenate(
        [velocity[:, cx - 2:].reshape((6,) + enthalpy.shape[1:]), pressure[cx - 2:],
         enthalpy[cx - 1:], solvent[cx - 1:]], axis=0)
    wide_head = jnp.concatenate([pressure[0:5], porosity[0:5]], axis=0)
    wide_tail = jnp.concatenate([pressure[cx - 5:], porosity[cx - 5:]], axis=0)
    n_left, n_right = neighbours(narrow_head, narrow_tail)
    w_left, w_right = neighbours(wide_head, wide_tail)

    vel2 = jnp.concatenate(
        [n_left[0:6].reshape((3, 2) + enthalpy.shape[1:]), velocity,
         n_right[0:6].reshape((3, 2) + enthalpy.shape[1:])], axis=1)
    pres5 = jnp.concatenate([w_left[0:5], pressure, w_right[0:5]], axis=0)
    poro5 = jnp.concatenate([w_left[5:10], porosity, w_right[5:10]], axis=0)
    heat1 = jnp.concatenate([n_left[8:9], enthalpy, n_right[8:9]], axis=0)
    solv1 = jnp.concatenate([n_left[9:10], solvent, n_right[9:10]], axis=0)

    advance(None)
    advance(None)
    advance(None)
    advance(None)
    vel_star, source, heat_new, solv_new = stage_one(vel2, pres5, heat1, poro5, solv1, solid_mask)
    advance(vel_star)

    s_left, s_right = neighbours(source[0:4], source[cx - 4:])
    source4 = jnp.concatenate([s_left, source, s_right], axis=0)
    advance(source4)

    velocity_new, final = stage_two(pres5, poro5, source4, vel_star)
    while zone_bits or duct_bits:
        advance(final)
    totals = state["totals"]
    gathered = state["buffer"][:rows]

    counts = zone_sizes.astype(jnp.float32) * (cx * enthalpy.shape[2])
    means = totals / counts
    fresh_all = means / (means + solvent_limit)
    fresh = jnp.sum(choose * fresh_all)
    target = jnp.sum(choose * zone_setpoint)
    arrived = lax.dynamic_index_in_dim(gathered, duct_source[0], axis=0, keepdims=False)
    supply_heat = (1.0 - fresh) * arrived[0] + fresh * target
    supply_solv = (1.0 - fresh) * arrived[1]
    column = jnp.arange(enthalpy.shape[2], dtype=jnp.int32)
    inside_box = (column >= duct_span[0, 0]) & (column < duct_span[0, 0] + duct_span[0, 1])
    jets = (nozzle_mask > 0) & inside_box[None, :]
    heat_layer = jnp.where(jets, supply_heat, heat_new[:, 0, :])
    solv_layer = jnp.where(jets, supply_solv, solv_new[:, 0, :])
    enthalpy_new = jnp.concatenate([heat_layer[:, None, :], heat_new[:, 1:, :]], axis=1)
    solvent_new = jnp.concatenate([solv_layer[:, None, :], solv_new[:, 1:, :]], axis=1)
    return (velocity_new, enthalpy_new, solvent_new, final)


def solution(mesh):
    placed = (
        P(None, ALL, None, None),
        P(ALL, None, None),
        P(ALL, None, None),
        P(ALL, None, None),
        P(ALL, None, None),
        P(ALL, None, None),
        P(ALL, None),
        P(),
        P(),
        P(ALL),
        P(ALL, None),
    )
    return jax.shard_map(
        on_device_body,
        mesh=mesh,
        in_specs=placed,
        out_specs=(
            P(None, ALL, None, None),
            P(ALL, None, None),
            P(ALL, None, None),
            P(ALL, None, None),
        ),
        check_vma=False,
    )
```

```python
import jax
import jax.numpy as jnp
from jax import lax
from jax.experimental import pallas as pl
from jax.experimental.pallas import tpu as pltpu
from jax.sharding import PartitionSpec as P

ITERS = 4
ALL = ("zone", "brick")


time_step = 0.2
viscosity = 0.1
diffusivity = 0.1
buoyancy = 0.5
evaporation = 0.5
latent_heat = 0.8
solvent_limit = 0.2


def neighbours(head, tail):
    count = lax.axis_size(ALL)
    from_left = lax.ppermute(tail, ALL, [(i, i + 1) for i in range(count - 1)])
    from_right = lax.ppermute(head, ALL, [(i + 1, i) for i in range(count - 1)])
    return from_left, from_right


def _down(v, axis):
    idx = lax.broadcasted_iota(jnp.int32, v.shape, axis)
    return jnp.where(idx == 0, 0.0, pltpu.roll(v, 1, axis))


def _up(v, axis):
    n = v.shape[axis]
    idx = lax.broadcasted_iota(jnp.int32, v.shape, axis)
    return jnp.where(idx == n - 1, 0.0, pltpu.roll(v, n - 1, axis))


def _laplacian_plane(back, centre, front):
    lap = back + front + _down(centre, 0) + _up(centre, 0)
    return lap + _down(centre, 1) + _up(centre, 1) - 6.0 * centre


def stage_one_kernel(velocity, pressure, enthalpy, solvent, porosity, solid, left, right,
                     star_out, source_out, heat_out, solv_out,
                     vel2, pres2, heat1, solv1, poro1, star):
    wide = star.shape[1]
    cells = source_out.shape[0]
    for component in range(3):
        vel2[component, 0:2] = left[2 * component:2 * component + 2]
        vel2[component, 2:cells + 2] = velocity[component]
        vel2[component, cells + 2:cells + 4] = right[2 * component:2 * component + 2]
    pres2[0:2] = left[6:8]
    pres2[2:cells + 2] = pressure[...]
    pres2[cells + 2:cells + 4] = right[6:8]
    for layer, (target, local) in enumerate(((heat1, enthalpy), (solv1, solvent), (poro1, porosity))):
        target[0:1] = left[8 + layer:9 + layer]
        target[1:cells + 1] = local[...]
        target[cells + 1:cells + 2] = right[8 + layer:9 + layer]

    def momentum_plane(j, carry):
        open_here = poro1[j]
        pressure_mid = pres2[j + 1]
        for component in range(3):
            centre = vel2[component, j + 1]
            laplacian = _laplacian_plane(vel2[component, j], centre, vel2[component, j + 2])
            if component == 0:
                gradient = 0.5 * (pres2[j + 2] - pres2[j])
            else:
                axis = component - 1
                gradient = 0.5 * (_up(pressure_mid, axis) - _down(pressure_mid, axis))
            forcing = viscosity * laplacian - gradient
            if component == 1:
                forcing = forcing + buoyancy * heat1[j]
            star[component, j] = open_here * (centre + time_step * forcing)
        return carry

    lax.fori_loop(0, wide, momentum_plane, 0)

    def cell_plane(x, carry):
        j = x + 1
        s0 = star[0, j]
        s1 = star[1, j]
        s2 = star[2, j]
        result = 0.5 * (star[0, j + 1] - star[0, j - 1])
        result = result + 0.5 * (_up(s1, 0) - _down(s1, 0))
        result = result + 0.5 * (_up(s2, 1) - _down(s2, 1))
        source_out[x] = result / time_step
        star_out[0, x] = s0
        star_out[1, x] = s1
        star_out[2, x] = s2
        drying = time_step * evaporation * solid[x].astype(jnp.float32) * solv1[j]
        for scalar, out, latent in ((heat1, heat_out, True), (solv1, solv_out, False)):
            back = scalar[x]
            centre = scalar[j]
            front = scalar[x + 2]
            laplacian = _laplacian_plane(back, centre, front)
            advect = jnp.maximum(s0, 0.0) * (centre - back) + jnp.minimum(s0, 0.0) * (front - centre)
            advect = advect + jnp.maximum(s1, 0.0) * (centre - _down(centre, 0))
            advect = advect + jnp.minimum(s1, 0.0) * (_up(centre, 0) - centre)
            advect = advect + jnp.maximum(s2, 0.0) * (centre - _down(centre, 1))
            advect = advect + jnp.minimum(s2, 0.0) * (_up(centre, 1) - centre)
            moved = centre + time_step * (diffusivity * laplacian - advect)
            if latent:
                out[x] = moved - latent_heat * drying
            else:
                out[x] = moved - drying
        return carry

    lax.fori_loop(0, cells, cell_plane, 0)


def stage_two_kernel(pressure, porosity, source, star_in, wide_left, wide_right,
                     source_left, source_right, vel_out, pres_out,
                     pres5, poro5, source4, even, odd):
    cells = pres_out.shape[0]
    pres5[0:5] = wide_left[0:5]
    pres5[5:cells + 5] = pressure[...]
    pres5[cells + 5:cells + 10] = wide_right[0:5]
    poro5[0:5] = wide_left[5:10]
    poro5[5:cells + 5] = porosity[...]
    poro5[cells + 5:cells + 10] = wide_right[5:10]
    source4[0:4] = source_left[...]
    source4[4:cells + 4] = source[...]
    source4[cells + 4:cells + 8] = source_right[...]
    buffers = (even, odd)
    prev = pres5
    for k in range(ITERS):
        out = buffers[k % 2]
        count = source4.shape[0] - 2 * k

        def body(j, carry, k=k, prev=prev, out=out):
            open_here = poro5[k + j + 1]
            pressure_mid = prev[j + 1]
            face_back = 0.5 * (open_here + poro5[k + j])
            face_front = 0.5 * (open_here + poro5[k + j + 2])
            numerator = face_back * prev[j] + face_front * prev[j + 2] - source4[k + j]
            denominator = face_back + face_front
            for axis in (0, 1):
                face_low = 0.5 * (open_here + _down(open_here, axis))
                face_high = 0.5 * (open_here + _up(open_here, axis))
                numerator = (
                    numerator
                    + face_low * _down(pressure_mid, axis)
                    + face_high * _up(pressure_mid, axis)
                )
                denominator = denominator + face_low + face_high
            inside = open_here > 0.0
            out[j] = jnp.where(inside, numerator / jnp.where(inside, denominator, 1.0), 0.0)
            return carry

        lax.fori_loop(0, count, body, 0)
        prev = out
    final = prev

    def finish(x, carry):
        here = final[x + 1]
        pres_out[x] = here
        scale = time_step * poro5[x + 5]
        vel_out[0, x] = star_in[0, x] - scale * (0.5 * (final[x + 2] - final[x]))
        vel_out[1, x] = star_in[1, x] - scale * (0.5 * (_up(here, 0) - _down(here, 0)))
        vel_out[2, x] = star_in[2, x] - scale * (0.5 * (_up(here, 1) - _down(here, 1)))
        return carry

    lax.fori_loop(0, cells, finish, 0)


def _params():
    return pltpu.CompilerParams(vmem_limit_bytes=48 * 1024 * 1024)


def stage_one(velocity, pressure, enthalpy, solvent, porosity, solid, left, right):
    cells = solid.shape[0]
    plane = solid.shape[1:]
    f32 = jnp.float32
    outs = (
        jax.ShapeDtypeStruct((3, cells) + plane, f32),
        jax.ShapeDtypeStruct((cells,) + plane, f32),
        jax.ShapeDtypeStruct((cells,) + plane, f32),
        jax.ShapeDtypeStruct((cells,) + plane, f32),
    )
    points = cells * plane[0] * plane[1]
    return pl.pallas_call(
        stage_one_kernel,
        out_shape=outs,
        scratch_shapes=[
            pltpu.VMEM((3, cells + 4) + plane, f32),
            pltpu.VMEM((cells + 4,) + plane, f32),
            pltpu.VMEM((cells + 2,) + plane, f32),
            pltpu.VMEM((cells + 2,) + plane, f32),
            pltpu.VMEM((cells + 2,) + plane, f32),
            pltpu.VMEM((3, cells + 2) + plane, f32),
        ],
        compiler_params=_params(),
        cost_estimate=pl.CostEstimate(
            flops=260 * points, transcendentals=0, bytes_accessed=4 * points * 19),
    )(velocity, pressure, enthalpy, solvent, porosity, solid, left, right)


def stage_two(pressure, porosity, source, vel_star, wide_left, wide_right, source_left,
              source_right):
    cells = vel_star.shape[1]
    plane = vel_star.shape[2:]
    f32 = jnp.float32
    outs = (
        jax.ShapeDtypeStruct((3, cells) + plane, f32),
        jax.ShapeDtypeStruct((cells,) + plane, f32),
    )
    points = cells * plane[0] * plane[1]
    return pl.pallas_call(
        stage_two_kernel,
        out_shape=outs,
        scratch_shapes=[
            pltpu.VMEM((cells + 10,) + plane, f32),
            pltpu.VMEM((cells + 10,) + plane, f32),
            pltpu.VMEM((cells + 8,) + plane, f32),
            pltpu.VMEM((cells + 8,) + plane, f32),
            pltpu.VMEM((cells + 8,) + plane, f32),
        ],
        compiler_params=_params(),
        cost_estimate=pl.CostEstimate(
            flops=200 * points, transcendentals=0, bytes_accessed=4 * points * 12),
    )(pressure, porosity, source, vel_star, wide_left, wide_right, source_left, source_right)


def on_device_body(
    velocity,
    enthalpy,
    solvent,
    pressure,
    porosity,
    solid_mask,
    nozzle_mask,
    zone_sizes,
    zone_setpoint,
    duct_source,
    duct_span,
):
    cx = enthalpy.shape[0]
    device = lax.axis_index(ALL)

    starts = jnp.cumsum(zone_sizes) - zone_sizes
    zone_here = jnp.sum((device >= starts).astype(jnp.int32)) - 1
    nzones = zone_sizes.shape[0]
    choose = (jnp.arange(nzones, dtype=jnp.int32) == zone_here).astype(jnp.float32)
    totals = choose * jnp.sum(solvent[:, -1, :])
    count = lax.axis_size(ALL)
    rows = lax.axis_size("zone")

    planes = jnp.stack([enthalpy[:, -1, :], solvent[:, -1, :]])
    buffer = jnp.zeros((rows + 1,) + planes.shape, jnp.float32)
    buffer = lax.dynamic_update_slice(
        buffer, planes[None], (lax.axis_index("zone"), 0, 0, 0)
    )
    buffer = buffer.at[rows, 0, 0, :nzones].set(totals)
    bricks = count // rows
    duct_bits = []
    bit = 1
    while bit < rows:
        duct_bits.append(bit)
        bit *= 2
    zone_bits = []
    bit = 1
    while bit < bricks:
        zone_bits.append(bit)
        bit *= 2
    state = {"buffer": buffer, "totals": None}

    def advance(anchor):
        if duct_bits:
            b = duct_bits.pop(0)
            key = "buffer"
            sent = lax.ppermute(
                state[key], "zone", [(i, i ^ b) for i in range(rows)])
        elif zone_bits:
            b = zone_bits.pop(0)
            key = "totals"
            if state[key] is None:
                state[key] = state["buffer"][rows, 0, 0, :nzones]
            sent = lax.ppermute(
                state[key], "brick", [(i, i ^ b) for i in range(bricks)])
        else:
            return
        if anchor is not None:
            sent, _ = lax.optimization_barrier((sent, anchor))
        state[key] = state[key] + sent

    plane = enthalpy.shape[1:]
    narrow_head = jnp.concatenate(
        [velocity[:, 0:2].reshape((6,) + plane), pressure[0:2],
         enthalpy[0:1], solvent[0:1], porosity[0:1]], axis=0)
    narrow_tail = jnp.concatenate(
        [velocity[:, cx - 2:].reshape((6,) + plane), pressure[cx - 2:],
         enthalpy[cx - 1:], solvent[cx - 1:], porosity[cx - 1:]], axis=0)
    wide_head = jnp.concatenate([pressure[0:5], porosity[0:5]], axis=0)
    wide_tail = jnp.concatenate([pressure[cx - 5:], porosity[cx - 5:]], axis=0)
    n_left, n_right = neighbours(narrow_head, narrow_tail)
    w_left, w_right = neighbours(wide_head, wide_tail)

    advance(None)
    advance(None)
    advance(None)
    advance(None)
    vel_star, source, heat_new, solv_new = stage_one(
        velocity, pressure, enthalpy, solvent, porosity, solid_mask, n_left, n_right)
    advance(vel_star)

    s_left, s_right = neighbours(source[0:4], source[cx - 4:])
    advance(s_left)

    velocity_new, final = stage_two(
        pressure, porosity, source, vel_star, w_left, w_right, s_left, s_right)
    while zone_bits or duct_bits:
        advance(final)
    totals = state["totals"]
    gathered = state["buffer"][:rows]

    counts = zone_sizes.astype(jnp.float32) * (cx * enthalpy.shape[2])
    means = totals / counts
    fresh_all = means / (means + solvent_limit)
    fresh = jnp.sum(choose * fresh_all)
    target = jnp.sum(choose * zone_setpoint)
    arrived = lax.dynamic_index_in_dim(gathered, duct_source[0], axis=0, keepdims=False)
    supply_heat = (1.0 - fresh) * arrived[0] + fresh * target
    supply_solv = (1.0 - fresh) * arrived[1]
    column = jnp.arange(enthalpy.shape[2], dtype=jnp.int32)
    inside_box = (column >= duct_span[0, 0]) & (column < duct_span[0, 0] + duct_span[0, 1])
    jets = (nozzle_mask > 0) & inside_box[None, :]
    heat_layer = jnp.where(jets, supply_heat, heat_new[:, 0, :])
    solv_layer = jnp.where(jets, supply_solv, solv_new[:, 0, :])
    enthalpy_new = jnp.concatenate([heat_layer[:, None, :], heat_new[:, 1:, :]], axis=1)
    solvent_new = jnp.concatenate([solv_layer[:, None, :], solv_new[:, 1:, :]], axis=1)
    return (velocity_new, enthalpy_new, solvent_new, final)


def solution(mesh):
    placed = (
        P(None, ALL, None, None),
        P(ALL, None, None),
        P(ALL, None, None),
        P(ALL, None, None),
        P(ALL, None, None),
        P(ALL, None, None),
        P(ALL, None),
        P(),
        P(),
        P(ALL),
        P(ALL, None),
    )
    return jax.shard_map(
        on_device_body,
        mesh=mesh,
        in_specs=placed,
        out_specs=(
            P(None, ALL, None, None),
            P(ALL, None, None),
            P(ALL, None, None),
            P(ALL, None, None),
        ),
        check_vma=False,
    )
```

```python
import jax
import jax.numpy as jnp
from jax import lax
from jax.experimental import pallas as pl
from jax.experimental.pallas import tpu as pltpu
from jax.sharding import PartitionSpec as P

ITERS = 4
ALL = ("zone", "brick")


time_step = 0.2
viscosity = 0.1
diffusivity = 0.1
buoyancy = 0.5
evaporation = 0.5
latent_heat = 0.8
solvent_limit = 0.2


def neighbours(head, tail):
    count = lax.axis_size(ALL)
    from_left = lax.ppermute(tail, ALL, [(i, i + 1) for i in range(count - 1)])
    from_right = lax.ppermute(head, ALL, [(i + 1, i) for i in range(count - 1)])
    return from_left, from_right


def _down(v, axis):
    idx = lax.broadcasted_iota(jnp.int32, v.shape, axis)
    return jnp.where(idx == 0, 0.0, pltpu.roll(v, 1, axis))


def _up(v, axis):
    n = v.shape[axis]
    idx = lax.broadcasted_iota(jnp.int32, v.shape, axis)
    return jnp.where(idx == n - 1, 0.0, pltpu.roll(v, n - 1, axis))


def _laplacian_plane(back, centre, front):
    lap = back + front + _down(centre, 0) + _up(centre, 0)
    return lap + _down(centre, 1) + _up(centre, 1) - 6.0 * centre


def stage_one_kernel(velocity, pressure, enthalpy, solvent, porosity, solid, left, right,
                     star_out, source_out, heat_out, solv_out,
                     vel2, pres2, heat1, solv1, poro1, star):
    wide = star.shape[1]
    cells = source_out.shape[0]
    for component in range(3):
        vel2[component, 0:2] = left[2 * component:2 * component + 2]
        vel2[component, 2:cells + 2] = velocity[component]
        vel2[component, cells + 2:cells + 4] = right[2 * component:2 * component + 2]
    pres2[0:2] = left[6:8]
    pres2[2:cells + 2] = pressure[...]
    pres2[cells + 2:cells + 4] = right[6:8]
    for layer, (target, local) in enumerate(((heat1, enthalpy), (solv1, solvent), (poro1, porosity))):
        target[0:1] = left[8 + layer:9 + layer]
        target[1:cells + 1] = local[...]
        target[cells + 1:cells + 2] = right[8 + layer:9 + layer]

    def momentum_plane(j, carry):
        open_here = poro1[j]
        pressure_mid = pres2[j + 1]
        for component in range(3):
            centre = vel2[component, j + 1]
            laplacian = _laplacian_plane(vel2[component, j], centre, vel2[component, j + 2])
            if component == 0:
                gradient = 0.5 * (pres2[j + 2] - pres2[j])
            else:
                axis = component - 1
                gradient = 0.5 * (_up(pressure_mid, axis) - _down(pressure_mid, axis))
            forcing = viscosity * laplacian - gradient
            if component == 1:
                forcing = forcing + buoyancy * heat1[j]
            star[component, j] = open_here * (centre + time_step * forcing)
        return carry

    lax.fori_loop(0, wide, momentum_plane, 0)

    def cell_plane(x, carry):
        j = x + 1
        s0 = star[0, j]
        s1 = star[1, j]
        s2 = star[2, j]
        result = 0.5 * (star[0, j + 1] - star[0, j - 1])
        result = result + 0.5 * (_up(s1, 0) - _down(s1, 0))
        result = result + 0.5 * (_up(s2, 1) - _down(s2, 1))
        source_out[x] = result / time_step
        star_out[0, x] = s0
        star_out[1, x] = s1
        star_out[2, x] = s2
        drying = time_step * evaporation * solid[x].astype(jnp.float32) * solv1[j]
        for scalar, out, latent in ((heat1, heat_out, True), (solv1, solv_out, False)):
            back = scalar[x]
            centre = scalar[j]
            front = scalar[x + 2]
            laplacian = _laplacian_plane(back, centre, front)
            advect = jnp.maximum(s0, 0.0) * (centre - back) + jnp.minimum(s0, 0.0) * (front - centre)
            advect = advect + jnp.maximum(s1, 0.0) * (centre - _down(centre, 0))
            advect = advect + jnp.minimum(s1, 0.0) * (_up(centre, 0) - centre)
            advect = advect + jnp.maximum(s2, 0.0) * (centre - _down(centre, 1))
            advect = advect + jnp.minimum(s2, 0.0) * (_up(centre, 1) - centre)
            moved = centre + time_step * (diffusivity * laplacian - advect)
            if latent:
                out[x] = moved - latent_heat * drying
            else:
                out[x] = moved - drying
        return carry

    lax.fori_loop(0, cells, cell_plane, 0)


def stage_two_kernel(pressure, porosity, source, star_in, wide_left, wide_right,
                     source_left, source_right, vel_out, pres_out,
                     pres5, poro5, source4, even, odd):
    cells = pres_out.shape[0]
    pres5[0:5] = wide_left[0:5]
    pres5[5:cells + 5] = pressure[...]
    pres5[cells + 5:cells + 10] = wide_right[0:5]
    poro5[0:5] = wide_left[5:10]
    poro5[5:cells + 5] = porosity[...]
    poro5[cells + 5:cells + 10] = wide_right[5:10]
    source4[0:4] = source_left[...]
    source4[4:cells + 4] = source[...]
    source4[cells + 4:cells + 8] = source_right[...]
    buffers = (even, odd)
    prev = pres5
    for k in range(ITERS):
        out = buffers[k % 2]
        count = source4.shape[0] - 2 * k

        def body(j, carry, k=k, prev=prev, out=out):
            open_here = poro5[k + j + 1]
            pressure_mid = prev[j + 1]
            face_back = 0.5 * (open_here + poro5[k + j])
            face_front = 0.5 * (open_here + poro5[k + j + 2])
            numerator = face_back * prev[j] + face_front * prev[j + 2] - source4[k + j]
            denominator = face_back + face_front
            for axis in (0, 1):
                face_low = 0.5 * (open_here + _down(open_here, axis))
                face_high = 0.5 * (open_here + _up(open_here, axis))
                numerator = (
                    numerator
                    + face_low * _down(pressure_mid, axis)
                    + face_high * _up(pressure_mid, axis)
                )
                denominator = denominator + face_low + face_high
            inside = open_here > 0.0
            out[j] = jnp.where(inside, numerator / jnp.where(inside, denominator, 1.0), 0.0)
            return carry

        lax.fori_loop(0, count, body, 0)
        prev = out
    final = prev

    def finish(x, carry):
        here = final[x + 1]
        pres_out[x] = here
        scale = time_step * poro5[x + 5]
        vel_out[0, x] = star_in[0, x] - scale * (0.5 * (final[x + 2] - final[x]))
        vel_out[1, x] = star_in[1, x] - scale * (0.5 * (_up(here, 0) - _down(here, 0)))
        vel_out[2, x] = star_in[2, x] - scale * (0.5 * (_up(here, 1) - _down(here, 1)))
        return carry

    lax.fori_loop(0, cells, finish, 0)


def _params():
    return pltpu.CompilerParams(vmem_limit_bytes=48 * 1024 * 1024)


def stage_one(velocity, pressure, enthalpy, solvent, porosity, solid, left, right):
    cells = solid.shape[0]
    plane = solid.shape[1:]
    f32 = jnp.float32
    outs = (
        jax.ShapeDtypeStruct((3, cells) + plane, f32),
        jax.ShapeDtypeStruct((cells,) + plane, f32),
        jax.ShapeDtypeStruct((cells,) + plane, f32),
        jax.ShapeDtypeStruct((cells,) + plane, f32),
    )
    points = cells * plane[0] * plane[1]
    return pl.pallas_call(
        stage_one_kernel,
        out_shape=outs,
        scratch_shapes=[
            pltpu.VMEM((3, cells + 4) + plane, f32),
            pltpu.VMEM((cells + 4,) + plane, f32),
            pltpu.VMEM((cells + 2,) + plane, f32),
            pltpu.VMEM((cells + 2,) + plane, f32),
            pltpu.VMEM((cells + 2,) + plane, f32),
            pltpu.VMEM((3, cells + 2) + plane, f32),
        ],
        compiler_params=_params(),
        cost_estimate=pl.CostEstimate(
            flops=260 * points, transcendentals=0, bytes_accessed=4 * points * 19),
    )(velocity, pressure, enthalpy, solvent, porosity, solid, left, right)


def stage_two(pressure, porosity, source, vel_star, wide_left, wide_right, source_left,
              source_right):
    cells = vel_star.shape[1]
    plane = vel_star.shape[2:]
    f32 = jnp.float32
    outs = (
        jax.ShapeDtypeStruct((3, cells) + plane, f32),
        jax.ShapeDtypeStruct((cells,) + plane, f32),
    )
    points = cells * plane[0] * plane[1]
    return pl.pallas_call(
        stage_two_kernel,
        out_shape=outs,
        scratch_shapes=[
            pltpu.VMEM((cells + 10,) + plane, f32),
            pltpu.VMEM((cells + 10,) + plane, f32),
            pltpu.VMEM((cells + 8,) + plane, f32),
            pltpu.VMEM((cells + 8,) + plane, f32),
            pltpu.VMEM((cells + 8,) + plane, f32),
        ],
        compiler_params=_params(),
        cost_estimate=pl.CostEstimate(
            flops=200 * points, transcendentals=0, bytes_accessed=4 * points * 12),
    )(pressure, porosity, source, vel_star, wide_left, wide_right, source_left, source_right)


def on_device_body(
    velocity,
    enthalpy,
    solvent,
    pressure,
    porosity,
    solid_mask,
    nozzle_mask,
    zone_sizes,
    zone_setpoint,
    duct_source,
    duct_span,
):
    cx = enthalpy.shape[0]
    device = lax.axis_index(ALL)

    starts = jnp.cumsum(zone_sizes) - zone_sizes
    zone_here = jnp.sum((device >= starts).astype(jnp.int32)) - 1
    nzones = zone_sizes.shape[0]
    choose = (jnp.arange(nzones, dtype=jnp.int32) == zone_here).astype(jnp.float32)
    totals = choose * jnp.sum(solvent[:, -1, :])
    count = lax.axis_size(ALL)
    rows = lax.axis_size("zone")

    planes = jnp.stack([enthalpy[:, -1, :], solvent[:, -1, :]])
    message = jnp.concatenate(
        [planes, jnp.zeros((1,) + planes.shape[1:], jnp.float32).at[0, 0, :nzones].set(totals)],
        axis=0)
    bricks = count // rows
    rounds = [("zone", rows, 1, rows)]
    stride = 1
    while stride < bricks:
        radix = 4 if stride * 4 <= bricks else bricks // stride
        rounds.append(("brick", bricks, stride, radix))
        stride *= radix
    state = {"totals": None, "arrived": None}

    def advance(anchor):
        if not rounds:
            return
        axis, size, stride, radix = rounds.pop(0)
        value = message if axis == "zone" else state["totals"]
        sent = [
            lax.ppermute(value, axis, [(i, i ^ (k * stride)) for i in range(size)])
            for k in range(1, radix)
        ]
        if anchor is not None:
            sent, _ = lax.optimization_barrier((sent, anchor))
        if axis == "zone":
            received = jnp.stack([message] + sent)
            pick = jnp.bitwise_xor(duct_source[0], lax.axis_index("zone"))
            state["arrived"] = lax.dynamic_index_in_dim(received, pick, axis=0, keepdims=False)
            state["totals"] = jnp.sum(received[:, 2, 0, :nzones], axis=0)
        else:
            total = state["totals"]
            for part in sent:
                total = total + part
            state["totals"] = total

    plane = enthalpy.shape[1:]
    narrow_head = jnp.concatenate(
        [velocity[:, 0:2].reshape((6,) + plane), pressure[0:2],
         enthalpy[0:1], solvent[0:1], porosity[0:1]], axis=0)
    narrow_tail = jnp.concatenate(
        [velocity[:, cx - 2:].reshape((6,) + plane), pressure[cx - 2:],
         enthalpy[cx - 1:], solvent[cx - 1:], porosity[cx - 1:]], axis=0)
    wide_head = jnp.concatenate([pressure[0:5], porosity[0:5]], axis=0)
    wide_tail = jnp.concatenate([pressure[cx - 5:], porosity[cx - 5:]], axis=0)
    n_left, n_right = neighbours(narrow_head, narrow_tail)
    w_left, w_right = neighbours(wide_head, wide_tail)

    advance(None)
    vel_star, source, heat_new, solv_new = stage_one(
        velocity, pressure, enthalpy, solvent, porosity, solid_mask, n_left, n_right)
    advance(vel_star)

    s_left, s_right = neighbours(source[0:4], source[cx - 4:])
    advance(s_left)
    advance(s_left)

    velocity_new, final = stage_two(
        pressure, porosity, source, vel_star, w_left, w_right, s_left, s_right)
    while rounds:
        advance(final)
    totals = state["totals"]
    arrived = state["arrived"]

    counts = zone_sizes.astype(jnp.float32) * (cx * enthalpy.shape[2])
    means = totals / counts
    fresh_all = means / (means + solvent_limit)
    fresh = jnp.sum(choose * fresh_all)
    target = jnp.sum(choose * zone_setpoint)
    supply_heat = (1.0 - fresh) * arrived[0] + fresh * target
    supply_solv = (1.0 - fresh) * arrived[1]
    column = jnp.arange(enthalpy.shape[2], dtype=jnp.int32)
    inside_box = (column >= duct_span[0, 0]) & (column < duct_span[0, 0] + duct_span[0, 1])
    jets = (nozzle_mask > 0) & inside_box[None, :]
    heat_layer = jnp.where(jets, supply_heat, heat_new[:, 0, :])
    solv_layer = jnp.where(jets, supply_solv, solv_new[:, 0, :])
    enthalpy_new = jnp.concatenate([heat_layer[:, None, :], heat_new[:, 1:, :]], axis=1)
    solvent_new = jnp.concatenate([solv_layer[:, None, :], solv_new[:, 1:, :]], axis=1)
    return (velocity_new, enthalpy_new, solvent_new, final)


def solution(mesh):
    placed = (
        P(None, ALL, None, None),
        P(ALL, None, None),
        P(ALL, None, None),
        P(ALL, None, None),
        P(ALL, None, None),
        P(ALL, None, None),
        P(ALL, None),
        P(),
        P(),
        P(ALL),
        P(ALL, None),
    )
    return jax.shard_map(
        on_device_body,
        mesh=mesh,
        in_specs=placed,
        out_specs=(
            P(None, ALL, None, None),
            P(ALL, None, None),
            P(ALL, None, None),
            P(ALL, None, None),
        ),
        check_vma=False,
    )
```

```python
import jax
import jax.numpy as jnp
from jax import lax
from jax.experimental import pallas as pl
from jax.experimental.pallas import tpu as pltpu
from jax.sharding import PartitionSpec as P

ITERS = 4
ALL = ("zone", "brick")


time_step = 0.2
viscosity = 0.1
diffusivity = 0.1
buoyancy = 0.5
evaporation = 0.5
latent_heat = 0.8
solvent_limit = 0.2


def neighbours(head, tail):
    count = lax.axis_size(ALL)
    from_left = lax.ppermute(tail, ALL, [(i, i + 1) for i in range(count - 1)])
    from_right = lax.ppermute(head, ALL, [(i + 1, i) for i in range(count - 1)])
    return from_left, from_right


def _down(v, axis):
    idx = lax.broadcasted_iota(jnp.int32, v.shape, axis)
    return jnp.where(idx == 0, 0.0, pltpu.roll(v, 1, axis))


def _up(v, axis):
    n = v.shape[axis]
    idx = lax.broadcasted_iota(jnp.int32, v.shape, axis)
    return jnp.where(idx == n - 1, 0.0, pltpu.roll(v, n - 1, axis))


def _laplacian_plane(back, centre, front):
    lap = back + front + _down(centre, 0) + _up(centre, 0)
    return lap + _down(centre, 1) + _up(centre, 1) - 6.0 * centre


def stage_one_kernel(velocity, pressure, enthalpy, solvent, porosity, solid, left, right,
                     star_out, source_out, heat_out, solv_out,
                     vel2, pres2, heat1, solv1, poro1, star):
    wide = star.shape[1]
    cells = source_out.shape[0]
    for component in range(3):
        vel2[component, 0:2] = left[2 * component:2 * component + 2]
        vel2[component, 2:cells + 2] = velocity[component]
        vel2[component, cells + 2:cells + 4] = right[2 * component:2 * component + 2]
    pres2[0:2] = left[6:8]
    pres2[2:cells + 2] = pressure[...]
    pres2[cells + 2:cells + 4] = right[6:8]
    for layer, (target, local) in enumerate(((heat1, enthalpy), (solv1, solvent), (poro1, porosity))):
        target[0:1] = left[8 + layer:9 + layer]
        target[1:cells + 1] = local[...]
        target[cells + 1:cells + 2] = right[8 + layer:9 + layer]

    def momentum_plane(j, carry):
        open_here = poro1[j]
        pressure_mid = pres2[j + 1]
        for component in range(3):
            centre = vel2[component, j + 1]
            laplacian = _laplacian_plane(vel2[component, j], centre, vel2[component, j + 2])
            if component == 0:
                gradient = 0.5 * (pres2[j + 2] - pres2[j])
            else:
                axis = component - 1
                gradient = 0.5 * (_up(pressure_mid, axis) - _down(pressure_mid, axis))
            forcing = viscosity * laplacian - gradient
            if component == 1:
                forcing = forcing + buoyancy * heat1[j]
            star[component, j] = open_here * (centre + time_step * forcing)
        return carry

    lax.fori_loop(0, wide, momentum_plane, 0)

    def cell_plane(x, carry):
        j = x + 1
        s0 = star[0, j]
        s1 = star[1, j]
        s2 = star[2, j]
        result = 0.5 * (star[0, j + 1] - star[0, j - 1])
        result = result + 0.5 * (_up(s1, 0) - _down(s1, 0))
        result = result + 0.5 * (_up(s2, 1) - _down(s2, 1))
        source_out[x] = result / time_step
        star_out[0, x] = s0
        star_out[1, x] = s1
        star_out[2, x] = s2
        drying = time_step * evaporation * solid[x].astype(jnp.float32) * solv1[j]
        for scalar, out, latent in ((heat1, heat_out, True), (solv1, solv_out, False)):
            back = scalar[x]
            centre = scalar[j]
            front = scalar[x + 2]
            laplacian = _laplacian_plane(back, centre, front)
            advect = jnp.maximum(s0, 0.0) * (centre - back) + jnp.minimum(s0, 0.0) * (front - centre)
            advect = advect + jnp.maximum(s1, 0.0) * (centre - _down(centre, 0))
            advect = advect + jnp.minimum(s1, 0.0) * (_up(centre, 0) - centre)
            advect = advect + jnp.maximum(s2, 0.0) * (centre - _down(centre, 1))
            advect = advect + jnp.minimum(s2, 0.0) * (_up(centre, 1) - centre)
            moved = centre + time_step * (diffusivity * laplacian - advect)
            if latent:
                out[x] = moved - latent_heat * drying
            else:
                out[x] = moved - drying
        return carry

    lax.fori_loop(0, cells, cell_plane, 0)


def stage_two_kernel(pressure, porosity, source, star_in, wide_left, wide_right,
                     source_left, source_right, vel_out, pres_out,
                     pres5, poro5, source4, even, odd):
    cells = pres_out.shape[0]
    pres5[0:5] = wide_left[0:5]
    pres5[5:cells + 5] = pressure[...]
    pres5[cells + 5:cells + 10] = wide_right[0:5]
    poro5[0:5] = wide_left[5:10]
    poro5[5:cells + 5] = porosity[...]
    poro5[cells + 5:cells + 10] = wide_right[5:10]
    source4[0:4] = source_left[...]
    source4[4:cells + 4] = source[...]
    source4[cells + 4:cells + 8] = source_right[...]
    buffers = (even, odd)
    prev = pres5
    for k in range(ITERS):
        out = buffers[k % 2]
        count = source4.shape[0] - 2 * k

        def body(j, carry, k=k, prev=prev, out=out):
            open_here = poro5[k + j + 1]
            pressure_mid = prev[j + 1]
            face_back = 0.5 * (open_here + poro5[k + j])
            face_front = 0.5 * (open_here + poro5[k + j + 2])
            numerator = face_back * prev[j] + face_front * prev[j + 2] - source4[k + j]
            denominator = face_back + face_front
            for axis in (0, 1):
                face_low = 0.5 * (open_here + _down(open_here, axis))
                face_high = 0.5 * (open_here + _up(open_here, axis))
                numerator = (
                    numerator
                    + face_low * _down(pressure_mid, axis)
                    + face_high * _up(pressure_mid, axis)
                )
                denominator = denominator + face_low + face_high
            inside = open_here > 0.0
            out[j] = jnp.where(inside, numerator / jnp.where(inside, denominator, 1.0), 0.0)
            return carry

        lax.fori_loop(0, count, body, 0)
        prev = out
    final = prev

    def finish(x, carry):
        here = final[x + 1]
        pres_out[x] = here
        scale = time_step * poro5[x + 5]
        vel_out[0, x] = star_in[0, x] - scale * (0.5 * (final[x + 2] - final[x]))
        vel_out[1, x] = star_in[1, x] - scale * (0.5 * (_up(here, 0) - _down(here, 0)))
        vel_out[2, x] = star_in[2, x] - scale * (0.5 * (_up(here, 1) - _down(here, 1)))
        return carry

    lax.fori_loop(0, cells, finish, 0)


def _params():
    return pltpu.CompilerParams(vmem_limit_bytes=48 * 1024 * 1024)


def stage_one(velocity, pressure, enthalpy, solvent, porosity, solid, left, right):
    cells = solid.shape[0]
    plane = solid.shape[1:]
    f32 = jnp.float32
    outs = (
        jax.ShapeDtypeStruct((3, cells) + plane, f32),
        jax.ShapeDtypeStruct((cells,) + plane, f32),
        jax.ShapeDtypeStruct((cells,) + plane, f32),
        jax.ShapeDtypeStruct((cells,) + plane, f32),
    )
    points = cells * plane[0] * plane[1]
    return pl.pallas_call(
        stage_one_kernel,
        out_shape=outs,
        scratch_shapes=[
            pltpu.VMEM((3, cells + 4) + plane, f32),
            pltpu.VMEM((cells + 4,) + plane, f32),
            pltpu.VMEM((cells + 2,) + plane, f32),
            pltpu.VMEM((cells + 2,) + plane, f32),
            pltpu.VMEM((cells + 2,) + plane, f32),
            pltpu.VMEM((3, cells + 2) + plane, f32),
        ],
        compiler_params=_params(),
        cost_estimate=pl.CostEstimate(
            flops=260 * points, transcendentals=0, bytes_accessed=4 * points * 19),
    )(velocity, pressure, enthalpy, solvent, porosity, solid, left, right)


def stage_two(pressure, porosity, source, vel_star, wide_left, wide_right, source_left,
              source_right):
    cells = vel_star.shape[1]
    plane = vel_star.shape[2:]
    f32 = jnp.float32
    outs = (
        jax.ShapeDtypeStruct((3, cells) + plane, f32),
        jax.ShapeDtypeStruct((cells,) + plane, f32),
    )
    points = cells * plane[0] * plane[1]
    return pl.pallas_call(
        stage_two_kernel,
        out_shape=outs,
        scratch_shapes=[
            pltpu.VMEM((cells + 10,) + plane, f32),
            pltpu.VMEM((cells + 10,) + plane, f32),
            pltpu.VMEM((cells + 8,) + plane, f32),
            pltpu.VMEM((cells + 8,) + plane, f32),
            pltpu.VMEM((cells + 8,) + plane, f32),
        ],
        compiler_params=_params(),
        cost_estimate=pl.CostEstimate(
            flops=200 * points, transcendentals=0, bytes_accessed=4 * points * 12),
    )(pressure, porosity, source, vel_star, wide_left, wide_right, source_left, source_right)


def on_device_body(
    velocity,
    enthalpy,
    solvent,
    pressure,
    porosity,
    solid_mask,
    nozzle_mask,
    zone_sizes,
    zone_setpoint,
    duct_source,
    duct_span,
):
    cx = enthalpy.shape[0]
    device = lax.axis_index(ALL)

    starts = jnp.cumsum(zone_sizes) - zone_sizes
    zone_here = jnp.sum((device >= starts).astype(jnp.int32)) - 1
    nzones = zone_sizes.shape[0]
    choose = (jnp.arange(nzones, dtype=jnp.int32) == zone_here).astype(jnp.float32)
    totals = choose * jnp.sum(solvent[:, -1, :])
    count = lax.axis_size(ALL)
    rows = lax.axis_size("zone")

    planes = jnp.stack([enthalpy[:, -1, :], solvent[:, -1, :]])
    message = jnp.concatenate(
        [planes, jnp.zeros((1,) + planes.shape[1:], jnp.float32).at[0, 0, :nzones].set(totals)],
        axis=0)
    bricks = count // rows
    rounds = [("zone", rows, 1, rows)]
    stride = 1
    while stride < bricks:
        radix = 4 if stride * 4 <= bricks else bricks // stride
        rounds.append(("brick", bricks, stride, radix))
        stride *= radix
    state = {"totals": None, "arrived": None}

    def advance(anchor):
        if not rounds:
            return
        axis, size, stride, radix = rounds.pop(0)
        value = message if axis == "zone" else state["totals"]
        sent = [
            lax.ppermute(value, axis, [(i, i ^ (k * stride)) for i in range(size)])
            for k in range(1, radix)
        ]
        if anchor is not None:
            sent, _ = lax.optimization_barrier((sent, anchor))
        if axis == "zone":
            pick = jnp.bitwise_xor(duct_source[0], lax.axis_index("zone"))
            arrived = message[0:2]
            total = message[2, 0, :nzones]
            for k, part in enumerate(sent, start=1):
                arrived = jnp.where(pick == k, part[0:2], arrived)
                total = total + part[2, 0, :nzones]
            state["arrived"] = arrived
            state["totals"] = total
        else:
            total = state["totals"]
            for part in sent:
                total = total + part
            state["totals"] = total

    plane = enthalpy.shape[1:]
    narrow_head = jnp.concatenate(
        [velocity[:, 0:2].reshape((6,) + plane), pressure[0:2],
         enthalpy[0:1], solvent[0:1], porosity[0:1]], axis=0)
    narrow_tail = jnp.concatenate(
        [velocity[:, cx - 2:].reshape((6,) + plane), pressure[cx - 2:],
         enthalpy[cx - 1:], solvent[cx - 1:], porosity[cx - 1:]], axis=0)
    wide_head = jnp.concatenate([pressure[0:5], porosity[0:5]], axis=0)
    wide_tail = jnp.concatenate([pressure[cx - 5:], porosity[cx - 5:]], axis=0)
    n_left, n_right = neighbours(narrow_head, narrow_tail)
    wide_head, wide_tail, _ = lax.optimization_barrier((wide_head, wide_tail, (n_left, n_right)))
    w_left, w_right = neighbours(wide_head, wide_tail)

    advance(None)
    vel_star, source, heat_new, solv_new = stage_one(
        velocity, pressure, enthalpy, solvent, porosity, solid_mask, n_left, n_right)
    advance(vel_star)

    s_left, s_right = neighbours(source[0:4], source[cx - 4:])
    advance(s_left)
    advance(s_left)

    velocity_new, final = stage_two(
        pressure, porosity, source, vel_star, w_left, w_right, s_left, s_right)
    while rounds:
        advance(final)
    totals = state["totals"]
    arrived = state["arrived"]

    counts = zone_sizes.astype(jnp.float32) * (cx * enthalpy.shape[2])
    means = totals / counts
    fresh_all = means / (means + solvent_limit)
    fresh = jnp.sum(choose * fresh_all)
    target = jnp.sum(choose * zone_setpoint)
    supply_heat = (1.0 - fresh) * arrived[0] + fresh * target
    supply_solv = (1.0 - fresh) * arrived[1]
    column = jnp.arange(enthalpy.shape[2], dtype=jnp.int32)
    inside_box = (column >= duct_span[0, 0]) & (column < duct_span[0, 0] + duct_span[0, 1])
    jets = (nozzle_mask > 0) & inside_box[None, :]
    heat_layer = jnp.where(jets, supply_heat, heat_new[:, 0, :])
    solv_layer = jnp.where(jets, supply_solv, solv_new[:, 0, :])
    enthalpy_new = jnp.concatenate([heat_layer[:, None, :], heat_new[:, 1:, :]], axis=1)
    solvent_new = jnp.concatenate([solv_layer[:, None, :], solv_new[:, 1:, :]], axis=1)
    return (velocity_new, enthalpy_new, solvent_new, final)


def solution(mesh):
    placed = (
        P(None, ALL, None, None),
        P(ALL, None, None),
        P(ALL, None, None),
        P(ALL, None, None),
        P(ALL, None, None),
        P(ALL, None, None),
        P(ALL, None),
        P(),
        P(),
        P(ALL),
        P(ALL, None),
    )
    return jax.shard_map(
        on_device_body,
        mesh=mesh,
        in_specs=placed,
        out_specs=(
            P(None, ALL, None, None),
            P(ALL, None, None),
            P(ALL, None, None),
            P(ALL, None, None),
        ),
        check_vma=False,
    )
```

```python
import jax
import jax.numpy as jnp
from jax import lax
from jax.experimental import pallas as pl
from jax.experimental.pallas import tpu as pltpu
from jax.sharding import PartitionSpec as P

ITERS = 4
ALL = ("zone", "brick")


time_step = 0.2
viscosity = 0.1
diffusivity = 0.1
buoyancy = 0.5
evaporation = 0.5
latent_heat = 0.8
solvent_limit = 0.2


def neighbours(head, tail):
    count = lax.axis_size(ALL)
    from_left = lax.ppermute(tail, ALL, [(i, i + 1) for i in range(count - 1)])
    from_right = lax.ppermute(head, ALL, [(i + 1, i) for i in range(count - 1)])
    return from_left, from_right


def _down(v, axis):
    idx = lax.broadcasted_iota(jnp.int32, v.shape, axis)
    return jnp.where(idx == 0, 0.0, pltpu.roll(v, 1, axis))


def _up(v, axis):
    n = v.shape[axis]
    idx = lax.broadcasted_iota(jnp.int32, v.shape, axis)
    return jnp.where(idx == n - 1, 0.0, pltpu.roll(v, n - 1, axis))


def _laplacian_plane(back, centre, front):
    lap = back + front + _down(centre, 0) + _up(centre, 0)
    return lap + _down(centre, 1) + _up(centre, 1) - 6.0 * centre


def stage_one_kernel(velocity, pressure, enthalpy, solvent, porosity, solid, left, right,
                     star_out, source_out, heat_out, solv_out,
                     vel2, pres2, heat1, solv1, poro1, star):
    wide = star.shape[1]
    cells = source_out.shape[0]
    for component in range(3):
        vel2[component, 0:2] = left[2 * component:2 * component + 2]
        vel2[component, 2:cells + 2] = velocity[component]
        vel2[component, cells + 2:cells + 4] = right[2 * component:2 * component + 2]
    pres2[0:2] = left[6:8]
    pres2[2:cells + 2] = pressure[...]
    pres2[cells + 2:cells + 4] = right[6:8]
    for layer, (target, local) in enumerate(((heat1, enthalpy), (solv1, solvent), (poro1, porosity))):
        target[0:1] = left[8 + layer:9 + layer]
        target[1:cells + 1] = local[...]
        target[cells + 1:cells + 2] = right[8 + layer:9 + layer]

    def momentum_plane(j, carry):
        open_here = poro1[j]
        pressure_mid = pres2[j + 1]
        for component in range(3):
            centre = vel2[component, j + 1]
            laplacian = _laplacian_plane(vel2[component, j], centre, vel2[component, j + 2])
            if component == 0:
                gradient = 0.5 * (pres2[j + 2] - pres2[j])
            else:
                axis = component - 1
                gradient = 0.5 * (_up(pressure_mid, axis) - _down(pressure_mid, axis))
            forcing = viscosity * laplacian - gradient
            if component == 1:
                forcing = forcing + buoyancy * heat1[j]
            star[component, j] = open_here * (centre + time_step * forcing)
        return carry

    lax.fori_loop(0, wide, momentum_plane, 0)

    def cell_plane(x, carry):
        j = x + 1
        s0 = star[0, j]
        s1 = star[1, j]
        s2 = star[2, j]
        result = 0.5 * (star[0, j + 1] - star[0, j - 1])
        result = result + 0.5 * (_up(s1, 0) - _down(s1, 0))
        result = result + 0.5 * (_up(s2, 1) - _down(s2, 1))
        source_out[x] = result / time_step
        star_out[0, x] = s0
        star_out[1, x] = s1
        star_out[2, x] = s2
        drying = time_step * evaporation * solid[x].astype(jnp.float32) * solv1[j]
        for scalar, out, latent in ((heat1, heat_out, True), (solv1, solv_out, False)):
            back = scalar[x]
            centre = scalar[j]
            front = scalar[x + 2]
            laplacian = _laplacian_plane(back, centre, front)
            advect = jnp.maximum(s0, 0.0) * (centre - back) + jnp.minimum(s0, 0.0) * (front - centre)
            advect = advect + jnp.maximum(s1, 0.0) * (centre - _down(centre, 0))
            advect = advect + jnp.minimum(s1, 0.0) * (_up(centre, 0) - centre)
            advect = advect + jnp.maximum(s2, 0.0) * (centre - _down(centre, 1))
            advect = advect + jnp.minimum(s2, 0.0) * (_up(centre, 1) - centre)
            moved = centre + time_step * (diffusivity * laplacian - advect)
            if latent:
                out[x] = moved - latent_heat * drying
            else:
                out[x] = moved - drying
        return carry

    lax.fori_loop(0, cells, cell_plane, 0)


def stage_two_kernel(pressure, porosity, source, star_in, wide_left, wide_right,
                     source_left, source_right, vel_out, pres_out,
                     pres5, poro5, source4, even, odd):
    cells = pres_out.shape[0]
    pres5[0:5] = wide_left[0:5]
    pres5[5:cells + 5] = pressure[...]
    pres5[cells + 5:cells + 10] = wide_right[0:5]
    poro5[0:5] = wide_left[5:10]
    poro5[5:cells + 5] = porosity[...]
    poro5[cells + 5:cells + 10] = wide_right[5:10]
    source4[0:4] = source_left[...]
    source4[4:cells + 4] = source[...]
    source4[cells + 4:cells + 8] = source_right[...]
    buffers = (even, odd)
    prev = pres5
    for k in range(ITERS):
        out = buffers[k % 2]
        count = source4.shape[0] - 2 * k

        def body(j, carry, k=k, prev=prev, out=out):
            open_here = poro5[k + j + 1]
            pressure_mid = prev[j + 1]
            face_back = 0.5 * (open_here + poro5[k + j])
            face_front = 0.5 * (open_here + poro5[k + j + 2])
            numerator = face_back * prev[j] + face_front * prev[j + 2] - source4[k + j]
            denominator = face_back + face_front
            for axis in (0, 1):
                face_low = 0.5 * (open_here + _down(open_here, axis))
                face_high = 0.5 * (open_here + _up(open_here, axis))
                numerator = (
                    numerator
                    + face_low * _down(pressure_mid, axis)
                    + face_high * _up(pressure_mid, axis)
                )
                denominator = denominator + face_low + face_high
            inside = open_here > 0.0
            out[j] = jnp.where(inside, numerator / jnp.where(inside, denominator, 1.0), 0.0)
            return carry

        lax.fori_loop(0, count, body, 0)
        prev = out
    final = prev

    def finish(x, carry):
        here = final[x + 1]
        pres_out[x] = here
        scale = time_step * poro5[x + 5]
        vel_out[0, x] = star_in[0, x] - scale * (0.5 * (final[x + 2] - final[x]))
        vel_out[1, x] = star_in[1, x] - scale * (0.5 * (_up(here, 0) - _down(here, 0)))
        vel_out[2, x] = star_in[2, x] - scale * (0.5 * (_up(here, 1) - _down(here, 1)))
        return carry

    lax.fori_loop(0, cells, finish, 0)


def _params():
    return pltpu.CompilerParams(vmem_limit_bytes=48 * 1024 * 1024)


def stage_one(velocity, pressure, enthalpy, solvent, porosity, solid, left, right):
    cells = solid.shape[0]
    plane = solid.shape[1:]
    f32 = jnp.float32
    outs = (
        jax.ShapeDtypeStruct((3, cells) + plane, f32),
        jax.ShapeDtypeStruct((cells,) + plane, f32),
        jax.ShapeDtypeStruct((cells,) + plane, f32),
        jax.ShapeDtypeStruct((cells,) + plane, f32),
    )
    points = cells * plane[0] * plane[1]
    return pl.pallas_call(
        stage_one_kernel,
        out_shape=outs,
        scratch_shapes=[
            pltpu.VMEM((3, cells + 4) + plane, f32),
            pltpu.VMEM((cells + 4,) + plane, f32),
            pltpu.VMEM((cells + 2,) + plane, f32),
            pltpu.VMEM((cells + 2,) + plane, f32),
            pltpu.VMEM((cells + 2,) + plane, f32),
            pltpu.VMEM((3, cells + 2) + plane, f32),
        ],
        compiler_params=_params(),
        cost_estimate=pl.CostEstimate(
            flops=260 * points, transcendentals=0, bytes_accessed=4 * points * 19),
    )(velocity, pressure, enthalpy, solvent, porosity, solid, left, right)


def stage_two(pressure, porosity, source, vel_star, wide_left, wide_right, source_left,
              source_right):
    cells = vel_star.shape[1]
    plane = vel_star.shape[2:]
    f32 = jnp.float32
    outs = (
        jax.ShapeDtypeStruct((3, cells) + plane, f32),
        jax.ShapeDtypeStruct((cells,) + plane, f32),
    )
    points = cells * plane[0] * plane[1]
    return pl.pallas_call(
        stage_two_kernel,
        out_shape=outs,
        scratch_shapes=[
            pltpu.VMEM((cells + 10,) + plane, f32),
            pltpu.VMEM((cells + 10,) + plane, f32),
            pltpu.VMEM((cells + 8,) + plane, f32),
            pltpu.VMEM((cells + 8,) + plane, f32),
            pltpu.VMEM((cells + 8,) + plane, f32),
        ],
        compiler_params=_params(),
        cost_estimate=pl.CostEstimate(
            flops=200 * points, transcendentals=0, bytes_accessed=4 * points * 12),
    )(pressure, porosity, source, vel_star, wide_left, wide_right, source_left, source_right)


def on_device_body(
    velocity,
    enthalpy,
    solvent,
    pressure,
    porosity,
    solid_mask,
    nozzle_mask,
    zone_sizes,
    zone_setpoint,
    duct_source,
    duct_span,
):
    cx = enthalpy.shape[0]
    device = lax.axis_index(ALL)

    starts = jnp.cumsum(zone_sizes) - zone_sizes
    zone_here = jnp.sum((device >= starts).astype(jnp.int32)) - 1
    nzones = zone_sizes.shape[0]
    choose = (jnp.arange(nzones, dtype=jnp.int32) == zone_here).astype(jnp.float32)
    totals = choose * jnp.sum(solvent[:, -1, :])
    count = lax.axis_size(ALL)
    rows = lax.axis_size("zone")

    planes = jnp.stack([enthalpy[:, -1, :], solvent[:, -1, :]])
    message = jnp.concatenate(
        [planes, jnp.zeros((1,) + planes.shape[1:], jnp.float32).at[0, 0, :nzones].set(totals)],
        axis=0)
    bricks = count // rows
    rounds = [("zone", rows, 1, rows)]
    stride = 1
    while stride < bricks:
        radix = min(8 if stride == 1 else 4, bricks // stride)
        rounds.append(("brick", bricks, stride, radix))
        stride *= radix
    state = {"totals": None, "arrived": None}

    def advance(anchor):
        if not rounds:
            return
        axis, size, stride, radix = rounds.pop(0)
        value = message if axis == "zone" else state["totals"]
        sent = [
            lax.ppermute(value, axis, [(i, i ^ (k * stride)) for i in range(size)])
            for k in range(1, radix)
        ]
        if anchor is not None:
            sent, _ = lax.optimization_barrier((sent, anchor))
        if axis == "zone":
            pick = jnp.bitwise_xor(duct_source[0], lax.axis_index("zone"))
            arrived = message[0:2]
            total = message[2, 0, :nzones]
            for k, part in enumerate(sent, start=1):
                arrived = jnp.where(pick == k, part[0:2], arrived)
                total = total + part[2, 0, :nzones]
            state["arrived"] = arrived
            state["totals"] = total
        else:
            total = state["totals"]
            for part in sent:
                total = total + part
            state["totals"] = total

    plane = enthalpy.shape[1:]
    narrow_head = jnp.concatenate(
        [velocity[:, 0:2].reshape((6,) + plane), pressure[0:2],
         enthalpy[0:1], solvent[0:1], porosity[0:1]], axis=0)
    narrow_tail = jnp.concatenate(
        [velocity[:, cx - 2:].reshape((6,) + plane), pressure[cx - 2:],
         enthalpy[cx - 1:], solvent[cx - 1:], porosity[cx - 1:]], axis=0)
    wide_head = jnp.concatenate([pressure[0:5], porosity[0:5]], axis=0)
    wide_tail = jnp.concatenate([pressure[cx - 5:], porosity[cx - 5:]], axis=0)
    n_left, n_right = neighbours(narrow_head, narrow_tail)
    wide_head, wide_tail, _ = lax.optimization_barrier((wide_head, wide_tail, (n_left, n_right)))
    w_left, w_right = neighbours(wide_head, wide_tail)

    vel_star, source, heat_new, solv_new = stage_one(
        velocity, pressure, enthalpy, solvent, porosity, solid_mask, n_left, n_right)
    advance(vel_star)

    s_left, s_right = neighbours(source[0:4], source[cx - 4:])

    velocity_new, final = stage_two(
        pressure, porosity, source, vel_star, w_left, w_right, s_left, s_right)
    while rounds:
        advance(final)
    totals = state["totals"]
    arrived = state["arrived"]

    counts = zone_sizes.astype(jnp.float32) * (cx * enthalpy.shape[2])
    means = totals / counts
    fresh_all = means / (means + solvent_limit)
    fresh = jnp.sum(choose * fresh_all)
    target = jnp.sum(choose * zone_setpoint)
    supply_heat = (1.0 - fresh) * arrived[0] + fresh * target
    supply_solv = (1.0 - fresh) * arrived[1]
    column = jnp.arange(enthalpy.shape[2], dtype=jnp.int32)
    inside_box = (column >= duct_span[0, 0]) & (column < duct_span[0, 0] + duct_span[0, 1])
    jets = (nozzle_mask > 0) & inside_box[None, :]
    heat_layer = jnp.where(jets, supply_heat, heat_new[:, 0, :])
    solv_layer = jnp.where(jets, supply_solv, solv_new[:, 0, :])
    enthalpy_new = jnp.concatenate([heat_layer[:, None, :], heat_new[:, 1:, :]], axis=1)
    solvent_new = jnp.concatenate([solv_layer[:, None, :], solv_new[:, 1:, :]], axis=1)
    return (velocity_new, enthalpy_new, solvent_new, final)


def solution(mesh):
    placed = (
        P(None, ALL, None, None),
        P(ALL, None, None),
        P(ALL, None, None),
        P(ALL, None, None),
        P(ALL, None, None),
        P(ALL, None, None),
        P(ALL, None),
        P(),
        P(),
        P(ALL),
        P(ALL, None),
    )
    return jax.shard_map(
        on_device_body,
        mesh=mesh,
        in_specs=placed,
        out_specs=(
            P(None, ALL, None, None),
            P(ALL, None, None),
            P(ALL, None, None),
            P(ALL, None, None),
        ),
        check_vma=False,
    )
```

```python
import jax
import jax.numpy as jnp
from jax import lax
from jax.experimental import pallas as pl
from jax.experimental.pallas import tpu as pltpu
from jax.sharding import PartitionSpec as P

ITERS = 4
ALL = ("zone", "brick")


time_step = 0.2
viscosity = 0.1
diffusivity = 0.1
buoyancy = 0.5
evaporation = 0.5
latent_heat = 0.8
solvent_limit = 0.2


def neighbours(head, tail):
    count = lax.axis_size(ALL)
    from_left = lax.ppermute(tail, ALL, [(i, i + 1) for i in range(count - 1)])
    from_right = lax.ppermute(head, ALL, [(i + 1, i) for i in range(count - 1)])
    return from_left, from_right


def _down(v, axis):
    idx = lax.broadcasted_iota(jnp.int32, v.shape, axis)
    return jnp.where(idx == 0, 0.0, pltpu.roll(v, 1, axis))


def _up(v, axis):
    n = v.shape[axis]
    idx = lax.broadcasted_iota(jnp.int32, v.shape, axis)
    return jnp.where(idx == n - 1, 0.0, pltpu.roll(v, n - 1, axis))


def _laplacian_plane(back, centre, front):
    lap = back + front + _down(centre, 0) + _up(centre, 0)
    return lap + _down(centre, 1) + _up(centre, 1) - 6.0 * centre


def stage_one_kernel(velocity, pressure, enthalpy, solvent, porosity, solid, left, right,
                     star_out, source_out, heat_out, solv_out,
                     vel2, pres2, heat1, solv1, poro1, star):
    wide = star.shape[1]
    cells = source_out.shape[0]
    for component in range(3):
        vel2[component, 0:2] = left[2 * component:2 * component + 2]
        vel2[component, 2:cells + 2] = velocity[component]
        vel2[component, cells + 2:cells + 4] = right[2 * component:2 * component + 2]
    pres2[0:2] = left[6:8]
    pres2[2:cells + 2] = pressure[...]
    pres2[cells + 2:cells + 4] = right[6:8]
    for layer, (target, local) in enumerate(((heat1, enthalpy), (solv1, solvent), (poro1, porosity))):
        target[0:1] = left[8 + layer:9 + layer]
        target[1:cells + 1] = local[...]
        target[cells + 1:cells + 2] = right[8 + layer:9 + layer]

    def momentum_plane(j, carry):
        open_here = poro1[j]
        pressure_mid = pres2[j + 1]
        for component in range(3):
            centre = vel2[component, j + 1]
            laplacian = _laplacian_plane(vel2[component, j], centre, vel2[component, j + 2])
            if component == 0:
                gradient = 0.5 * (pres2[j + 2] - pres2[j])
            else:
                axis = component - 1
                gradient = 0.5 * (_up(pressure_mid, axis) - _down(pressure_mid, axis))
            forcing = viscosity * laplacian - gradient
            if component == 1:
                forcing = forcing + buoyancy * heat1[j]
            star[component, j] = open_here * (centre + time_step * forcing)
        return carry

    lax.fori_loop(0, wide, momentum_plane, 0)

    def cell_plane(x, carry):
        j = x + 1
        s0 = star[0, j]
        s1 = star[1, j]
        s2 = star[2, j]
        result = 0.5 * (star[0, j + 1] - star[0, j - 1])
        result = result + 0.5 * (_up(s1, 0) - _down(s1, 0))
        result = result + 0.5 * (_up(s2, 1) - _down(s2, 1))
        source_out[x] = result / time_step
        star_out[0, x] = s0
        star_out[1, x] = s1
        star_out[2, x] = s2
        drying = time_step * evaporation * solid[x].astype(jnp.float32) * solv1[j]
        for scalar, out, latent in ((heat1, heat_out, True), (solv1, solv_out, False)):
            back = scalar[x]
            centre = scalar[j]
            front = scalar[x + 2]
            laplacian = _laplacian_plane(back, centre, front)
            advect = jnp.maximum(s0, 0.0) * (centre - back) + jnp.minimum(s0, 0.0) * (front - centre)
            advect = advect + jnp.maximum(s1, 0.0) * (centre - _down(centre, 0))
            advect = advect + jnp.minimum(s1, 0.0) * (_up(centre, 0) - centre)
            advect = advect + jnp.maximum(s2, 0.0) * (centre - _down(centre, 1))
            advect = advect + jnp.minimum(s2, 0.0) * (_up(centre, 1) - centre)
            moved = centre + time_step * (diffusivity * laplacian - advect)
            if latent:
                out[x] = moved - latent_heat * drying
            else:
                out[x] = moved - drying
        return carry

    lax.fori_loop(0, cells, cell_plane, 0)


def stage_two_kernel(pressure, porosity, source, star_in, wide_left, wide_right,
                     source_left, source_right, vel_out, pres_out,
                     pres5, poro5, source4, even, odd):
    cells = pres_out.shape[0]
    pres5[0:5] = wide_left[0:5]
    pres5[5:cells + 5] = pressure[...]
    pres5[cells + 5:cells + 10] = wide_right[0:5]
    poro5[0:5] = wide_left[5:10]
    poro5[5:cells + 5] = porosity[...]
    poro5[cells + 5:cells + 10] = wide_right[5:10]
    source4[0:4] = source_left[...]
    source4[4:cells + 4] = source[...]
    source4[cells + 4:cells + 8] = source_right[...]
    buffers = (even, odd)
    prev = pres5
    for k in range(ITERS):
        out = buffers[k % 2]
        count = source4.shape[0] - 2 * k

        def body(j, carry, k=k, prev=prev, out=out):
            open_here = poro5[k + j + 1]
            pressure_mid = prev[j + 1]
            face_back = 0.5 * (open_here + poro5[k + j])
            face_front = 0.5 * (open_here + poro5[k + j + 2])
            numerator = face_back * prev[j] + face_front * prev[j + 2] - source4[k + j]
            denominator = face_back + face_front
            for axis in (0, 1):
                face_low = 0.5 * (open_here + _down(open_here, axis))
                face_high = 0.5 * (open_here + _up(open_here, axis))
                numerator = (
                    numerator
                    + face_low * _down(pressure_mid, axis)
                    + face_high * _up(pressure_mid, axis)
                )
                denominator = denominator + face_low + face_high
            inside = open_here > 0.0
            out[j] = jnp.where(inside, numerator / jnp.where(inside, denominator, 1.0), 0.0)
            return carry

        lax.fori_loop(0, count, body, 0)
        prev = out
    final = prev

    def finish(x, carry):
        here = final[x + 1]
        pres_out[x] = here
        scale = time_step * poro5[x + 5]
        vel_out[0, x] = star_in[0, x] - scale * (0.5 * (final[x + 2] - final[x]))
        vel_out[1, x] = star_in[1, x] - scale * (0.5 * (_up(here, 0) - _down(here, 0)))
        vel_out[2, x] = star_in[2, x] - scale * (0.5 * (_up(here, 1) - _down(here, 1)))
        return carry

    lax.fori_loop(0, cells, finish, 0)


def _params():
    return pltpu.CompilerParams(vmem_limit_bytes=48 * 1024 * 1024)


def stage_one(velocity, pressure, enthalpy, solvent, porosity, solid, left, right):
    cells = solid.shape[0]
    plane = solid.shape[1:]
    f32 = jnp.float32
    outs = (
        jax.ShapeDtypeStruct((3, cells) + plane, f32),
        jax.ShapeDtypeStruct((cells,) + plane, f32),
        jax.ShapeDtypeStruct((cells,) + plane, f32),
        jax.ShapeDtypeStruct((cells,) + plane, f32),
    )
    points = cells * plane[0] * plane[1]
    return pl.pallas_call(
        stage_one_kernel,
        out_shape=outs,
        scratch_shapes=[
            pltpu.VMEM((3, cells + 4) + plane, f32),
            pltpu.VMEM((cells + 4,) + plane, f32),
            pltpu.VMEM((cells + 2,) + plane, f32),
            pltpu.VMEM((cells + 2,) + plane, f32),
            pltpu.VMEM((cells + 2,) + plane, f32),
            pltpu.VMEM((3, cells + 2) + plane, f32),
        ],
        compiler_params=_params(),
        cost_estimate=pl.CostEstimate(
            flops=260 * points, transcendentals=0, bytes_accessed=4 * points * 19),
    )(velocity, pressure, enthalpy, solvent, porosity, solid, left, right)


def stage_two(pressure, porosity, source, vel_star, wide_left, wide_right, source_left,
              source_right):
    cells = vel_star.shape[1]
    plane = vel_star.shape[2:]
    f32 = jnp.float32
    outs = (
        jax.ShapeDtypeStruct((3, cells) + plane, f32),
        jax.ShapeDtypeStruct((cells,) + plane, f32),
    )
    points = cells * plane[0] * plane[1]
    return pl.pallas_call(
        stage_two_kernel,
        out_shape=outs,
        scratch_shapes=[
            pltpu.VMEM((cells + 10,) + plane, f32),
            pltpu.VMEM((cells + 10,) + plane, f32),
            pltpu.VMEM((cells + 8,) + plane, f32),
            pltpu.VMEM((cells + 8,) + plane, f32),
            pltpu.VMEM((cells + 8,) + plane, f32),
        ],
        compiler_params=_params(),
        cost_estimate=pl.CostEstimate(
            flops=200 * points, transcendentals=0, bytes_accessed=4 * points * 12),
    )(pressure, porosity, source, vel_star, wide_left, wide_right, source_left, source_right)


def on_device_body(
    velocity,
    enthalpy,
    solvent,
    pressure,
    porosity,
    solid_mask,
    nozzle_mask,
    zone_sizes,
    zone_setpoint,
    duct_source,
    duct_span,
):
    cx = enthalpy.shape[0]
    device = lax.axis_index(ALL)

    starts = jnp.cumsum(zone_sizes) - zone_sizes
    zone_here = jnp.sum((device >= starts).astype(jnp.int32)) - 1
    nzones = zone_sizes.shape[0]
    choose = (jnp.arange(nzones, dtype=jnp.int32) == zone_here).astype(jnp.float32)
    totals = choose * jnp.sum(solvent[:, -1, :])
    count = lax.axis_size(ALL)
    rows = lax.axis_size("zone")

    planes = jnp.stack([enthalpy[:, -1, :], solvent[:, -1, :]])
    bricks = count // rows
    rounds = []
    stride = 1
    while stride < bricks:
        radix = min(8 if stride == 1 else 4, bricks // stride)
        rounds.append(("brick", bricks, stride, radix))
        stride *= radix
    rounds.append(("zone", rows, 1, rows))
    state = {"totals": totals, "arrived": None}

    def advance(anchor):
        if not rounds:
            return
        axis, size, stride, radix = rounds.pop(0)
        if axis == "zone":
            carried = jnp.zeros((1,) + planes.shape[1:], jnp.float32)
            carried = carried.at[0, 0, :nzones].set(state["totals"])
            message = jnp.concatenate([planes, carried], axis=0)
            value = message
        else:
            value = state["totals"]
        sent = [
            lax.ppermute(value, axis, [(i, i ^ (k * stride)) for i in range(size)])
            for k in range(1, radix)
        ]
        if anchor is not None:
            sent, _ = lax.optimization_barrier((sent, anchor))
        if axis == "zone":
            pick = jnp.bitwise_xor(duct_source[0], lax.axis_index("zone"))
            arrived = message[0:2]
            total = message[2, 0, :nzones]
            for k, part in enumerate(sent, start=1):
                arrived = jnp.where(pick == k, part[0:2], arrived)
                total = total + part[2, 0, :nzones]
            state["arrived"] = arrived
            state["totals"] = total
        else:
            total = state["totals"]
            for part in sent:
                total = total + part
            state["totals"] = total

    advance(None)
    advance(None)
    advance(None)

    plane = enthalpy.shape[1:]
    narrow_head = jnp.concatenate(
        [velocity[:, 0:2].reshape((6,) + plane), pressure[0:2],
         enthalpy[0:1], solvent[0:1], porosity[0:1]], axis=0)
    narrow_tail = jnp.concatenate(
        [velocity[:, cx - 2:].reshape((6,) + plane), pressure[cx - 2:],
         enthalpy[cx - 1:], solvent[cx - 1:], porosity[cx - 1:]], axis=0)
    wide_head = jnp.concatenate([pressure[0:5], porosity[0:5]], axis=0)
    wide_tail = jnp.concatenate([pressure[cx - 5:], porosity[cx - 5:]], axis=0)
    n_left, n_right = neighbours(narrow_head, narrow_tail)
    wide_head, wide_tail, _ = lax.optimization_barrier((wide_head, wide_tail, (n_left, n_right)))
    w_left, w_right = neighbours(wide_head, wide_tail)

    vel_star, source, heat_new, solv_new = stage_one(
        velocity, pressure, enthalpy, solvent, porosity, solid_mask, n_left, n_right)

    s_left, s_right = neighbours(source[0:4], source[cx - 4:])

    velocity_new, final = stage_two(
        pressure, porosity, source, vel_star, w_left, w_right, s_left, s_right)
    while rounds:
        advance(final)
    totals = state["totals"]
    arrived = state["arrived"]

    counts = zone_sizes.astype(jnp.float32) * (cx * enthalpy.shape[2])
    means = totals / counts
    fresh_all = means / (means + solvent_limit)
    fresh = jnp.sum(choose * fresh_all)
    target = jnp.sum(choose * zone_setpoint)
    supply_heat = (1.0 - fresh) * arrived[0] + fresh * target
    supply_solv = (1.0 - fresh) * arrived[1]
    column = jnp.arange(enthalpy.shape[2], dtype=jnp.int32)
    inside_box = (column >= duct_span[0, 0]) & (column < duct_span[0, 0] + duct_span[0, 1])
    jets = (nozzle_mask > 0) & inside_box[None, :]
    heat_layer = jnp.where(jets, supply_heat, heat_new[:, 0, :])
    solv_layer = jnp.where(jets, supply_solv, solv_new[:, 0, :])
    enthalpy_new = jnp.concatenate([heat_layer[:, None, :], heat_new[:, 1:, :]], axis=1)
    solvent_new = jnp.concatenate([solv_layer[:, None, :], solv_new[:, 1:, :]], axis=1)
    return (velocity_new, enthalpy_new, solvent_new, final)


def solution(mesh):
    placed = (
        P(None, ALL, None, None),
        P(ALL, None, None),
        P(ALL, None, None),
        P(ALL, None, None),
        P(ALL, None, None),
        P(ALL, None, None),
        P(ALL, None),
        P(),
        P(),
        P(ALL),
        P(ALL, None),
    )
    return jax.shard_map(
        on_device_body,
        mesh=mesh,
        in_specs=placed,
        out_specs=(
            P(None, ALL, None, None),
            P(ALL, None, None),
            P(ALL, None, None),
            P(ALL, None, None),
        ),
        check_vma=False,
    )
```

```python
import jax
import jax.numpy as jnp
from jax import lax
from jax.experimental import pallas as pl
from jax.experimental.pallas import tpu as pltpu
from jax.sharding import PartitionSpec as P

ITERS = 4
ALL = ("zone", "brick")


time_step = 0.2
viscosity = 0.1
diffusivity = 0.1
buoyancy = 0.5
evaporation = 0.5
latent_heat = 0.8
solvent_limit = 0.2


def neighbours(head, tail):
    count = lax.axis_size(ALL)
    from_left = lax.ppermute(tail, ALL, [(i, i + 1) for i in range(count - 1)])
    from_right = lax.ppermute(head, ALL, [(i + 1, i) for i in range(count - 1)])
    return from_left, from_right


def _down(v, axis):
    idx = lax.broadcasted_iota(jnp.int32, v.shape, axis)
    return jnp.where(idx == 0, 0.0, pltpu.roll(v, 1, axis))


def _up(v, axis):
    n = v.shape[axis]
    idx = lax.broadcasted_iota(jnp.int32, v.shape, axis)
    return jnp.where(idx == n - 1, 0.0, pltpu.roll(v, n - 1, axis))


def _laplacian_plane(back, centre, front):
    lap = back + front + _down(centre, 0) + _up(centre, 0)
    return lap + _down(centre, 1) + _up(centre, 1) - 6.0 * centre


def stage_one_kernel(velocity, pressure, enthalpy, solvent, porosity, solid, left, right,
                     star_out, source_out, heat_out, solv_out,
                     vel2, pres2, heat1, solv1, poro1, star):
    wide = star.shape[1]
    cells = source_out.shape[0]
    for component in range(3):
        vel2[component, 0:2] = left[2 * component:2 * component + 2]
        vel2[component, 2:cells + 2] = velocity[component]
        vel2[component, cells + 2:cells + 4] = right[2 * component:2 * component + 2]
    pres2[0:2] = left[6:8]
    pres2[2:cells + 2] = pressure[...]
    pres2[cells + 2:cells + 4] = right[6:8]
    for layer, (target, local) in enumerate(((heat1, enthalpy), (solv1, solvent), (poro1, porosity))):
        target[0:1] = left[8 + layer:9 + layer]
        target[1:cells + 1] = local[...]
        target[cells + 1:cells + 2] = right[8 + layer:9 + layer]

    def momentum_plane(j, carry):
        open_here = poro1[j]
        pressure_mid = pres2[j + 1]
        for component in range(3):
            centre = vel2[component, j + 1]
            laplacian = _laplacian_plane(vel2[component, j], centre, vel2[component, j + 2])
            if component == 0:
                gradient = 0.5 * (pres2[j + 2] - pres2[j])
            else:
                axis = component - 1
                gradient = 0.5 * (_up(pressure_mid, axis) - _down(pressure_mid, axis))
            forcing = viscosity * laplacian - gradient
            if component == 1:
                forcing = forcing + buoyancy * heat1[j]
            star[component, j] = open_here * (centre + time_step * forcing)
        return carry

    lax.fori_loop(0, wide, momentum_plane, 0)

    def cell_plane(x, carry):
        j = x + 1
        s0 = star[0, j]
        s1 = star[1, j]
        s2 = star[2, j]
        result = 0.5 * (star[0, j + 1] - star[0, j - 1])
        result = result + 0.5 * (_up(s1, 0) - _down(s1, 0))
        result = result + 0.5 * (_up(s2, 1) - _down(s2, 1))
        source_out[x] = result / time_step
        star_out[0, x] = s0
        star_out[1, x] = s1
        star_out[2, x] = s2
        drying = time_step * evaporation * solid[x].astype(jnp.float32) * solv1[j]
        for scalar, out, latent in ((heat1, heat_out, True), (solv1, solv_out, False)):
            back = scalar[x]
            centre = scalar[j]
            front = scalar[x + 2]
            laplacian = _laplacian_plane(back, centre, front)
            advect = jnp.maximum(s0, 0.0) * (centre - back) + jnp.minimum(s0, 0.0) * (front - centre)
            advect = advect + jnp.maximum(s1, 0.0) * (centre - _down(centre, 0))
            advect = advect + jnp.minimum(s1, 0.0) * (_up(centre, 0) - centre)
            advect = advect + jnp.maximum(s2, 0.0) * (centre - _down(centre, 1))
            advect = advect + jnp.minimum(s2, 0.0) * (_up(centre, 1) - centre)
            moved = centre + time_step * (diffusivity * laplacian - advect)
            if latent:
                out[x] = moved - latent_heat * drying
            else:
                out[x] = moved - drying
        return carry

    lax.fori_loop(0, cells, cell_plane, 0)


def stage_two_kernel(pressure, porosity, source, star_in, wide_left, wide_right,
                     source_left, source_right, left, right, vel_out, pres_out,
                     pres5, poro5, source4, even, odd):
    cells = pres_out.shape[0]
    pres5[0:3] = wide_left[0:3]
    pres5[3:5] = left[6:8]
    pres5[5:cells + 5] = pressure[...]
    pres5[cells + 5:cells + 7] = right[6:8]
    pres5[cells + 7:cells + 10] = wide_right[0:3]
    poro5[0:4] = wide_left[3:7]
    poro5[4:5] = left[10:11]
    poro5[5:cells + 5] = porosity[...]
    poro5[cells + 5:cells + 6] = right[10:11]
    poro5[cells + 6:cells + 10] = wide_right[3:7]
    source4[0:4] = source_left[...]
    source4[4:cells + 4] = source[...]
    source4[cells + 4:cells + 8] = source_right[...]
    buffers = (even, odd)
    prev = pres5
    for k in range(ITERS):
        out = buffers[k % 2]
        count = source4.shape[0] - 2 * k

        def body(j, carry, k=k, prev=prev, out=out):
            open_here = poro5[k + j + 1]
            pressure_mid = prev[j + 1]
            face_back = 0.5 * (open_here + poro5[k + j])
            face_front = 0.5 * (open_here + poro5[k + j + 2])
            numerator = face_back * prev[j] + face_front * prev[j + 2] - source4[k + j]
            denominator = face_back + face_front
            for axis in (0, 1):
                face_low = 0.5 * (open_here + _down(open_here, axis))
                face_high = 0.5 * (open_here + _up(open_here, axis))
                numerator = (
                    numerator
                    + face_low * _down(pressure_mid, axis)
                    + face_high * _up(pressure_mid, axis)
                )
                denominator = denominator + face_low + face_high
            inside = open_here > 0.0
            out[j] = jnp.where(inside, numerator / jnp.where(inside, denominator, 1.0), 0.0)
            return carry

        lax.fori_loop(0, count, body, 0)
        prev = out
    final = prev

    def finish(x, carry):
        here = final[x + 1]
        pres_out[x] = here
        scale = time_step * poro5[x + 5]
        vel_out[0, x] = star_in[0, x] - scale * (0.5 * (final[x + 2] - final[x]))
        vel_out[1, x] = star_in[1, x] - scale * (0.5 * (_up(here, 0) - _down(here, 0)))
        vel_out[2, x] = star_in[2, x] - scale * (0.5 * (_up(here, 1) - _down(here, 1)))
        return carry

    lax.fori_loop(0, cells, finish, 0)


def _params():
    return pltpu.CompilerParams(vmem_limit_bytes=48 * 1024 * 1024)


def stage_one(velocity, pressure, enthalpy, solvent, porosity, solid, left, right):
    cells = solid.shape[0]
    plane = solid.shape[1:]
    f32 = jnp.float32
    outs = (
        jax.ShapeDtypeStruct((3, cells) + plane, f32),
        jax.ShapeDtypeStruct((cells,) + plane, f32),
        jax.ShapeDtypeStruct((cells,) + plane, f32),
        jax.ShapeDtypeStruct((cells,) + plane, f32),
    )
    points = cells * plane[0] * plane[1]
    return pl.pallas_call(
        stage_one_kernel,
        out_shape=outs,
        scratch_shapes=[
            pltpu.VMEM((3, cells + 4) + plane, f32),
            pltpu.VMEM((cells + 4,) + plane, f32),
            pltpu.VMEM((cells + 2,) + plane, f32),
            pltpu.VMEM((cells + 2,) + plane, f32),
            pltpu.VMEM((cells + 2,) + plane, f32),
            pltpu.VMEM((3, cells + 2) + plane, f32),
        ],
        compiler_params=_params(),
        cost_estimate=pl.CostEstimate(
            flops=260 * points, transcendentals=0, bytes_accessed=4 * points * 19),
    )(velocity, pressure, enthalpy, solvent, porosity, solid, left, right)


def stage_two(pressure, porosity, source, vel_star, wide_left, wide_right, source_left,
              source_right, left, right):
    cells = vel_star.shape[1]
    plane = vel_star.shape[2:]
    f32 = jnp.float32
    outs = (
        jax.ShapeDtypeStruct((3, cells) + plane, f32),
        jax.ShapeDtypeStruct((cells,) + plane, f32),
    )
    points = cells * plane[0] * plane[1]
    return pl.pallas_call(
        stage_two_kernel,
        out_shape=outs,
        scratch_shapes=[
            pltpu.VMEM((cells + 10,) + plane, f32),
            pltpu.VMEM((cells + 10,) + plane, f32),
            pltpu.VMEM((cells + 8,) + plane, f32),
            pltpu.VMEM((cells + 8,) + plane, f32),
            pltpu.VMEM((cells + 8,) + plane, f32),
        ],
        compiler_params=_params(),
        cost_estimate=pl.CostEstimate(
            flops=200 * points, transcendentals=0, bytes_accessed=4 * points * 12),
    )(pressure, porosity, source, vel_star, wide_left, wide_right, source_left, source_right,
      left, right)


def on_device_body(
    velocity,
    enthalpy,
    solvent,
    pressure,
    porosity,
    solid_mask,
    nozzle_mask,
    zone_sizes,
    zone_setpoint,
    duct_source,
    duct_span,
):
    cx = enthalpy.shape[0]
    device = lax.axis_index(ALL)

    starts = jnp.cumsum(zone_sizes) - zone_sizes
    zone_here = jnp.sum((device >= starts).astype(jnp.int32)) - 1
    nzones = zone_sizes.shape[0]
    choose = (jnp.arange(nzones, dtype=jnp.int32) == zone_here).astype(jnp.float32)
    totals = choose * jnp.sum(solvent[:, -1, :])
    count = lax.axis_size(ALL)
    rows = lax.axis_size("zone")

    planes = jnp.stack([enthalpy[:, -1, :], solvent[:, -1, :]])
    message = jnp.concatenate(
        [planes, jnp.zeros((1,) + planes.shape[1:], jnp.float32).at[0, 0, :nzones].set(totals)],
        axis=0)
    bricks = count // rows
    rounds = [("zone", rows, 1, rows)]
    stride = 1
    while stride < bricks:
        radix = 4 if stride * 4 <= bricks else bricks // stride
        rounds.append(("brick", bricks, stride, radix))
        stride *= radix
    state = {"totals": None, "arrived": None}

    def advance(anchor):
        if not rounds:
            return
        axis, size, stride, radix = rounds.pop(0)
        value = message if axis == "zone" else state["totals"]
        sent = [
            lax.ppermute(value, axis, [(i, i ^ (k * stride)) for i in range(size)])
            for k in range(1, radix)
        ]
        if anchor is not None:
            sent, _ = lax.optimization_barrier((sent, anchor))
        if axis == "zone":
            pick = jnp.bitwise_xor(duct_source[0], lax.axis_index("zone"))
            arrived = message[0:2]
            total = message[2, 0, :nzones]
            for k, part in enumerate(sent, start=1):
                arrived = jnp.where(pick == k, part[0:2], arrived)
                total = total + part[2, 0, :nzones]
            state["arrived"] = arrived
            state["totals"] = total
        else:
            total = state["totals"]
            for part in sent:
                total = total + part
            state["totals"] = total

    plane = enthalpy.shape[1:]
    narrow_head = jnp.concatenate(
        [velocity[:, 0:2].reshape((6,) + plane), pressure[0:2],
         enthalpy[0:1], solvent[0:1], porosity[0:1]], axis=0)
    narrow_tail = jnp.concatenate(
        [velocity[:, cx - 2:].reshape((6,) + plane), pressure[cx - 2:],
         enthalpy[cx - 1:], solvent[cx - 1:], porosity[cx - 1:]], axis=0)
    wide_head = jnp.concatenate([pressure[2:5], porosity[1:5]], axis=0)
    wide_tail = jnp.concatenate([pressure[cx - 5:cx - 2], porosity[cx - 5:cx - 1]], axis=0)
    n_left, n_right = neighbours(narrow_head, narrow_tail)
    wide_head, wide_tail, _ = lax.optimization_barrier((wide_head, wide_tail, (n_left, n_right)))
    w_left, w_right = neighbours(wide_head, wide_tail)

    advance(None)
    vel_star, source, heat_new, solv_new = stage_one(
        velocity, pressure, enthalpy, solvent, porosity, solid_mask, n_left, n_right)
    advance(vel_star)

    s_left, s_right = neighbours(source[0:4], source[cx - 4:])
    advance(s_left)
    advance(s_left)

    velocity_new, final = stage_two(
        pressure, porosity, source, vel_star, w_left, w_right, s_left, s_right,
        n_left, n_right)
    while rounds:
        advance(final)
    totals = state["totals"]
    arrived = state["arrived"]

    counts = zone_sizes.astype(jnp.float32) * (cx * enthalpy.shape[2])
    means = totals / counts
    fresh_all = means / (means + solvent_limit)
    fresh = jnp.sum(choose * fresh_all)
    target = jnp.sum(choose * zone_setpoint)
    supply_heat = (1.0 - fresh) * arrived[0] + fresh * target
    supply_solv = (1.0 - fresh) * arrived[1]
    column = jnp.arange(enthalpy.shape[2], dtype=jnp.int32)
    inside_box = (column >= duct_span[0, 0]) & (column < duct_span[0, 0] + duct_span[0, 1])
    jets = (nozzle_mask > 0) & inside_box[None, :]
    heat_layer = jnp.where(jets, supply_heat, heat_new[:, 0, :])
    solv_layer = jnp.where(jets, supply_solv, solv_new[:, 0, :])
    enthalpy_new = jnp.concatenate([heat_layer[:, None, :], heat_new[:, 1:, :]], axis=1)
    solvent_new = jnp.concatenate([solv_layer[:, None, :], solv_new[:, 1:, :]], axis=1)
    return (velocity_new, enthalpy_new, solvent_new, final)


def solution(mesh):
    placed = (
        P(None, ALL, None, None),
        P(ALL, None, None),
        P(ALL, None, None),
        P(ALL, None, None),
        P(ALL, None, None),
        P(ALL, None, None),
        P(ALL, None),
        P(),
        P(),
        P(ALL),
        P(ALL, None),
    )
    return jax.shard_map(
        on_device_body,
        mesh=mesh,
        in_specs=placed,
        out_specs=(
            P(None, ALL, None, None),
            P(ALL, None, None),
            P(ALL, None, None),
            P(ALL, None, None),
        ),
        check_vma=False,
    )
```

```python
import jax
import jax.numpy as jnp
from jax import lax
from jax.experimental import pallas as pl
from jax.experimental.pallas import tpu as pltpu
from jax.sharding import PartitionSpec as P

ITERS = 4
ALL = ("zone", "brick")


time_step = 0.2
viscosity = 0.1
diffusivity = 0.1
buoyancy = 0.5
evaporation = 0.5
latent_heat = 0.8
solvent_limit = 0.2


def neighbours(head, tail):
    count = lax.axis_size(ALL)
    from_left = lax.ppermute(tail, ALL, [(i, i + 1) for i in range(count - 1)])
    from_right = lax.ppermute(head, ALL, [(i + 1, i) for i in range(count - 1)])
    return from_left, from_right


def _down(v, axis):
    idx = lax.broadcasted_iota(jnp.int32, v.shape, axis)
    return jnp.where(idx == 0, 0.0, pltpu.roll(v, 1, axis))


def _up(v, axis):
    n = v.shape[axis]
    idx = lax.broadcasted_iota(jnp.int32, v.shape, axis)
    return jnp.where(idx == n - 1, 0.0, pltpu.roll(v, n - 1, axis))


def _laplacian_plane(back, centre, front):
    lap = back + front + _down(centre, 0) + _up(centre, 0)
    return lap + _down(centre, 1) + _up(centre, 1) - 6.0 * centre


def stage_one_kernel(velocity, pressure, enthalpy, solvent, porosity, solid, left, right,
                     star_out, source_out, heat_out, solv_out,
                     vel2, pres2, heat1, solv1, poro1, star):
    wide = star.shape[1]
    cells = source_out.shape[0]
    for component in range(3):
        vel2[component, 0:2] = left[2 * component:2 * component + 2]
        vel2[component, 2:cells + 2] = velocity[component]
        vel2[component, cells + 2:cells + 4] = right[2 * component:2 * component + 2]
    pres2[0:2] = left[6:8]
    pres2[2:cells + 2] = pressure[...]
    pres2[cells + 2:cells + 4] = right[6:8]
    for layer, (target, local) in enumerate(((heat1, enthalpy), (solv1, solvent), (poro1, porosity))):
        target[0:1] = left[8 + layer:9 + layer]
        target[1:cells + 1] = local[...]
        target[cells + 1:cells + 2] = right[8 + layer:9 + layer]

    def momentum_plane(j, carry):
        open_here = poro1[j]
        pressure_mid = pres2[j + 1]
        for component in range(3):
            centre = vel2[component, j + 1]
            laplacian = _laplacian_plane(vel2[component, j], centre, vel2[component, j + 2])
            if component == 0:
                gradient = 0.5 * (pres2[j + 2] - pres2[j])
            else:
                axis = component - 1
                gradient = 0.5 * (_up(pressure_mid, axis) - _down(pressure_mid, axis))
            forcing = viscosity * laplacian - gradient
            if component == 1:
                forcing = forcing + buoyancy * heat1[j]
            star[component, j] = open_here * (centre + time_step * forcing)
        return carry

    lax.fori_loop(0, wide, momentum_plane, 0)

    def cell_plane(x, carry):
        j = x + 1
        s0 = star[0, j]
        s1 = star[1, j]
        s2 = star[2, j]
        result = 0.5 * (star[0, j + 1] - star[0, j - 1])
        result = result + 0.5 * (_up(s1, 0) - _down(s1, 0))
        result = result + 0.5 * (_up(s2, 1) - _down(s2, 1))
        source_out[x] = result / time_step
        star_out[0, x] = s0
        star_out[1, x] = s1
        star_out[2, x] = s2
        drying = time_step * evaporation * solid[x].astype(jnp.float32) * solv1[j]
        for scalar, out, latent in ((heat1, heat_out, True), (solv1, solv_out, False)):
            back = scalar[x]
            centre = scalar[j]
            front = scalar[x + 2]
            laplacian = _laplacian_plane(back, centre, front)
            advect = jnp.maximum(s0, 0.0) * (centre - back) + jnp.minimum(s0, 0.0) * (front - centre)
            advect = advect + jnp.maximum(s1, 0.0) * (centre - _down(centre, 0))
            advect = advect + jnp.minimum(s1, 0.0) * (_up(centre, 0) - centre)
            advect = advect + jnp.maximum(s2, 0.0) * (centre - _down(centre, 1))
            advect = advect + jnp.minimum(s2, 0.0) * (_up(centre, 1) - centre)
            moved = centre + time_step * (diffusivity * laplacian - advect)
            if latent:
                out[x] = moved - latent_heat * drying
            else:
                out[x] = moved - drying
        return carry

    lax.fori_loop(0, cells, cell_plane, 0)


def stage_two_kernel(pressure, porosity, source, star_in, wide_left, wide_right,
                     source_left, source_right, vel_out, pres_out,
                     pres5, poro5, source4, even, odd, coef):
    cells = pres_out.shape[0]
    pres5[0:5] = wide_left[0:5]
    pres5[5:cells + 5] = pressure[...]
    pres5[cells + 5:cells + 10] = wide_right[0:5]
    poro5[0:5] = wide_left[5:10]
    poro5[5:cells + 5] = porosity[...]
    poro5[cells + 5:cells + 10] = wide_right[5:10]
    source4[0:4] = source_left[...]
    source4[4:cells + 4] = source[...]
    source4[cells + 4:cells + 8] = source_right[...]

    def faces(j, carry):
        open_here = poro5[j + 1]
        face_back = 0.5 * (open_here + poro5[j])
        face_front = 0.5 * (open_here + poro5[j + 2])
        coef[0, j] = face_back
        coef[1, j] = face_front
        denominator = face_back + face_front
        for axis in (0, 1):
            face_low = 0.5 * (open_here + _down(open_here, axis))
            face_high = 0.5 * (open_here + _up(open_here, axis))
            coef[2 + 2 * axis, j] = face_low
            coef[3 + 2 * axis, j] = face_high
            denominator = denominator + face_low + face_high
        coef[6, j] = denominator
        return carry

    lax.fori_loop(0, source4.shape[0], faces, 0)
    buffers = (even, odd)
    prev = pres5
    for k in range(ITERS):
        out = buffers[k % 2]
        count = source4.shape[0] - 2 * k

        def body(j, carry, k=k, prev=prev, out=out):
            c = k + j
            open_here = poro5[c + 1]
            pressure_mid = prev[j + 1]
            numerator = coef[0, c] * prev[j] + coef[1, c] * prev[j + 2] - source4[c]
            for axis in (0, 1):
                numerator = (
                    numerator
                    + coef[2 + 2 * axis, c] * _down(pressure_mid, axis)
                    + coef[3 + 2 * axis, c] * _up(pressure_mid, axis)
                )
            inside = open_here > 0.0
            out[j] = jnp.where(inside, numerator / jnp.where(inside, coef[6, c], 1.0), 0.0)
            return carry

        lax.fori_loop(0, count, body, 0)
        prev = out
    final = prev

    def finish(x, carry):
        here = final[x + 1]
        pres_out[x] = here
        scale = time_step * poro5[x + 5]
        vel_out[0, x] = star_in[0, x] - scale * (0.5 * (final[x + 2] - final[x]))
        vel_out[1, x] = star_in[1, x] - scale * (0.5 * (_up(here, 0) - _down(here, 0)))
        vel_out[2, x] = star_in[2, x] - scale * (0.5 * (_up(here, 1) - _down(here, 1)))
        return carry

    lax.fori_loop(0, cells, finish, 0)


def _params():
    return pltpu.CompilerParams(vmem_limit_bytes=48 * 1024 * 1024)


def stage_one(velocity, pressure, enthalpy, solvent, porosity, solid, left, right):
    cells = solid.shape[0]
    plane = solid.shape[1:]
    f32 = jnp.float32
    outs = (
        jax.ShapeDtypeStruct((3, cells) + plane, f32),
        jax.ShapeDtypeStruct((cells,) + plane, f32),
        jax.ShapeDtypeStruct((cells,) + plane, f32),
        jax.ShapeDtypeStruct((cells,) + plane, f32),
    )
    points = cells * plane[0] * plane[1]
    return pl.pallas_call(
        stage_one_kernel,
        out_shape=outs,
        scratch_shapes=[
            pltpu.VMEM((3, cells + 4) + plane, f32),
            pltpu.VMEM((cells + 4,) + plane, f32),
            pltpu.VMEM((cells + 2,) + plane, f32),
            pltpu.VMEM((cells + 2,) + plane, f32),
            pltpu.VMEM((cells + 2,) + plane, f32),
            pltpu.VMEM((3, cells + 2) + plane, f32),
        ],
        compiler_params=_params(),
        cost_estimate=pl.CostEstimate(
            flops=260 * points, transcendentals=0, bytes_accessed=4 * points * 19),
    )(velocity, pressure, enthalpy, solvent, porosity, solid, left, right)


def stage_two(pressure, porosity, source, vel_star, wide_left, wide_right, source_left,
              source_right):
    cells = vel_star.shape[1]
    plane = vel_star.shape[2:]
    f32 = jnp.float32
    outs = (
        jax.ShapeDtypeStruct((3, cells) + plane, f32),
        jax.ShapeDtypeStruct((cells,) + plane, f32),
    )
    points = cells * plane[0] * plane[1]
    return pl.pallas_call(
        stage_two_kernel,
        out_shape=outs,
        scratch_shapes=[
            pltpu.VMEM((cells + 10,) + plane, f32),
            pltpu.VMEM((cells + 10,) + plane, f32),
            pltpu.VMEM((cells + 8,) + plane, f32),
            pltpu.VMEM((cells + 8,) + plane, f32),
            pltpu.VMEM((cells + 8,) + plane, f32),
            pltpu.VMEM((7, cells + 8) + plane, f32),
        ],
        compiler_params=_params(),
        cost_estimate=pl.CostEstimate(
            flops=200 * points, transcendentals=0, bytes_accessed=4 * points * 12),
    )(pressure, porosity, source, vel_star, wide_left, wide_right, source_left, source_right)


def on_device_body(
    velocity,
    enthalpy,
    solvent,
    pressure,
    porosity,
    solid_mask,
    nozzle_mask,
    zone_sizes,
    zone_setpoint,
    duct_source,
    duct_span,
):
    cx = enthalpy.shape[0]
    device = lax.axis_index(ALL)

    starts = jnp.cumsum(zone_sizes) - zone_sizes
    zone_here = jnp.sum((device >= starts).astype(jnp.int32)) - 1
    nzones = zone_sizes.shape[0]
    choose = (jnp.arange(nzones, dtype=jnp.int32) == zone_here).astype(jnp.float32)
    totals = choose * jnp.sum(solvent[:, -1, :])
    count = lax.axis_size(ALL)
    rows = lax.axis_size("zone")

    planes = jnp.stack([enthalpy[:, -1, :], solvent[:, -1, :]])
    message = jnp.concatenate(
        [planes, jnp.zeros((1,) + planes.shape[1:], jnp.float32).at[0, 0, :nzones].set(totals)],
        axis=0)
    bricks = count // rows
    rounds = [("zone", rows, 1, rows)]
    stride = 1
    while stride < bricks:
        radix = 4 if stride * 4 <= bricks else bricks // stride
        rounds.append(("brick", bricks, stride, radix))
        stride *= radix
    state = {"totals": None, "arrived": None}

    def advance(anchor):
        if not rounds:
            return
        axis, size, stride, radix = rounds.pop(0)
        value = message if axis == "zone" else state["totals"]
        sent = [
            lax.ppermute(value, axis, [(i, i ^ (k * stride)) for i in range(size)])
            for k in range(1, radix)
        ]
        if anchor is not None:
            sent, _ = lax.optimization_barrier((sent, anchor))
        if axis == "zone":
            pick = jnp.bitwise_xor(duct_source[0], lax.axis_index("zone"))
            arrived = message[0:2]
            total = message[2, 0, :nzones]
            for k, part in enumerate(sent, start=1):
                arrived = jnp.where(pick == k, part[0:2], arrived)
                total = total + part[2, 0, :nzones]
            state["arrived"] = arrived
            state["totals"] = total
        else:
            total = state["totals"]
            for part in sent:
                total = total + part
            state["totals"] = total

    plane = enthalpy.shape[1:]
    narrow_head = jnp.concatenate(
        [velocity[:, 0:2].reshape((6,) + plane), pressure[0:2],
         enthalpy[0:1], solvent[0:1], porosity[0:1]], axis=0)
    narrow_tail = jnp.concatenate(
        [velocity[:, cx - 2:].reshape((6,) + plane), pressure[cx - 2:],
         enthalpy[cx - 1:], solvent[cx - 1:], porosity[cx - 1:]], axis=0)
    wide_head = jnp.concatenate([pressure[0:5], porosity[0:5]], axis=0)
    wide_tail = jnp.concatenate([pressure[cx - 5:], porosity[cx - 5:]], axis=0)
    n_left, n_right = neighbours(narrow_head, narrow_tail)
    wide_head, wide_tail, _ = lax.optimization_barrier((wide_head, wide_tail, (n_left, n_right)))
    w_left, w_right = neighbours(wide_head, wide_tail)

    advance(None)
    vel_star, source, heat_new, solv_new = stage_one(
        velocity, pressure, enthalpy, solvent, porosity, solid_mask, n_left, n_right)
    advance(vel_star)

    s_left, s_right = neighbours(source[0:4], source[cx - 4:])
    advance(s_left)
    advance(s_left)

    velocity_new, final = stage_two(
        pressure, porosity, source, vel_star, w_left, w_right, s_left, s_right)
    while rounds:
        advance(final)
    totals = state["totals"]
    arrived = state["arrived"]

    counts = zone_sizes.astype(jnp.float32) * (cx * enthalpy.shape[2])
    means = totals / counts
    fresh_all = means / (means + solvent_limit)
    fresh = jnp.sum(choose * fresh_all)
    target = jnp.sum(choose * zone_setpoint)
    supply_heat = (1.0 - fresh) * arrived[0] + fresh * target
    supply_solv = (1.0 - fresh) * arrived[1]
    column = jnp.arange(enthalpy.shape[2], dtype=jnp.int32)
    inside_box = (column >= duct_span[0, 0]) & (column < duct_span[0, 0] + duct_span[0, 1])
    jets = (nozzle_mask > 0) & inside_box[None, :]
    heat_layer = jnp.where(jets, supply_heat, heat_new[:, 0, :])
    solv_layer = jnp.where(jets, supply_solv, solv_new[:, 0, :])
    enthalpy_new = heat_new.at[:, 0, :].set(heat_layer)
    solvent_new = solv_new.at[:, 0, :].set(solv_layer)
    return (velocity_new, enthalpy_new, solvent_new, final)


def solution(mesh):
    placed = (
        P(None, ALL, None, None),
        P(ALL, None, None),
        P(ALL, None, None),
        P(ALL, None, None),
        P(ALL, None, None),
        P(ALL, None, None),
        P(ALL, None),
        P(),
        P(),
        P(ALL),
        P(ALL, None),
    )
    return jax.shard_map(
        on_device_body,
        mesh=mesh,
        in_specs=placed,
        out_specs=(
            P(None, ALL, None, None),
            P(ALL, None, None),
            P(ALL, None, None),
            P(ALL, None, None),
        ),
        check_vma=False,
    )
```
